32 devices in a mesh: videos: 2 (over y), group: 16 (over z, x, core).
Axes of the slice: x: 2, y: 2, z: 4, core: 2. Of those that a mesh axis runs over, the one named last changes fastest.
Arguments:
- queries: bfloat16 [4096, 3072], P(('videos', 'group')), parts along dimension 0, may hold values from -90 to 90
- fresh_keys: bfloat16 [4096, 3072], P(('videos', 'group')), parts along dimension 0, may hold values from -8.375 to 8.375
- fresh_values: bfloat16 [4096, 3072], P(('videos', 'group')), parts along dimension 0, may hold values from -6 to 6
- cache_keys: bfloat16 [64, 3072], P(('videos', 'group')), parts along dimension 0, may hold values from -9 to 9
- cache_values: bfloat16 [64, 3072], P(('videos', 'group')), parts along dimension 0, may hold values from -6 to 6
- lengths: int32 [32], P(('videos', 'group')), parts along dimension 0, may hold values from 1 to 128, 1228 in all
- levels: int32 [32], P(('videos', 'group')), parts along dimension 0, may hold values from 0 to 15
- gate_table: float32 [16, 3072], replicated, may hold values from -24 to 24
Outputs:
- modulated: bfloat16 [4096, 3072], P(('videos', 'group')), parts along dimension 0
The draws below stay inside these ranges and needn't reach their ends.
There are 2 independent parts, one for each index of `videos`. The reference program is written for one: setup_inputs(seed, part) draws one part's arguments, and reference() takes and returns one part's arrays. A program takes and returns all parts, laid end to end along the dimension named above; an argument that names none is the same for every part. Nothing has to cross between parts.
Inputs may be any that keep to these rules, and one draw needn't show every extreme that they name: Each video block has 128 slots, the first lengths of them live; the lengths sum to 1228 in each video; in every draw some block is full.
All inputs are finite; a program needn't handle non-finite values.
Results may differ from the reference program's by a relative error of at most 0.0045.
Values may be sent and summed in bfloat16 or wider, within the bound.
No kernel may reach another device: no remote copies, remote signals or barrier semaphores. Data moves between devices by JAX's collectives and lax.ppermute only.
A program may use at most 64 MiB of HBM per device.

```python
import math
import jax
import jax.numpy as jnp
import numpy as np
from jax import lax

HEADS = 24
HEAD_DIM = 128
TOK_DEV = 128
WIN = 4
CACHE_DEV = 2
LEVELS = 16
BLOCKS = 16
TOKENS = 2048
CACHE = 32


def draw_queries(key, part):
    row_count = TOK_DEV * BLOCKS
    noise = jax.random.normal(jax.random.fold_in(key, 11), (row_count, HEADS * HEAD_DIM), jnp.float32)
    noise = 1.4 * jnp.clip(noise, -6.0, 6.0)
    return noise.astype(jnp.bfloat16)


def draw_cache_keys(key, part):
    row_count = CACHE_DEV * BLOCKS
    noise = jax.random.normal(jax.random.fold_in(key, 21), (row_count, HEADS * HEAD_DIM), jnp.float32)
    noise = 1.4 * jnp.clip(noise, -6.0, 6.0)
    return noise.astype(jnp.bfloat16)


def plant(entries, own_key, least, largest):
    longest = entries.shape.index(max(entries.shape))
    spots = []
    for shift in (0, 1):
        where = [jax.random.randint(jax.random.fold_in(own_key, axis), (), 0, length) for axis, length in enumerate(entries.shape)]
        where[longest] = (where[longest] + shift) % entries.shape[longest]
        spots.append(tuple(where))
    return entries.at[spots[0]].set(least).at[spots[1]].set(largest)


def block_levels(rng, shape, cuts, low, largest):
    def one(axis_at, blocks):
        steps = jax.random.uniform(jax.random.fold_in(jax.random.fold_in(rng, 6), axis_at), (blocks,), jnp.float32, low / len(cuts), largest / len(cuts))
        return jnp.repeat(jnp.exp(steps), shape[axis_at] // blocks).reshape((-1,) + (1,) * (len(shape) - axis_at - 1))

    gain = one(*cuts[0])
    for cut in cuts[1:]:
        gain = gain * one(*cut)
    return gain


def split_up(number_of, total, bound, slope):
    loads = [(1 << 20) // math.isqrt(rank ** slope) + 1 for rank in range(2, number_of + 1)]
    rest, given = total - bound - (number_of - 1), [1] * (number_of - 1)
    while rest > 0:
        free = [i for i in range(number_of - 1) if given[i] < bound]
        mass, remaining = sum([loads[i] for i in free]), rest
        for i in free:
            addition = min(bound - given[i], max(1, remaining * loads[i] // mass), rest)
            given[i] = given[i] + addition
            rest = rest - addition
    return np.array([bound] + given)


def uneven_parts(key, number_of, total, most, lean):
    if number_of == 2:
        one = jax.random.randint(key, (), max(1, total - most), min(most, total - 1) + 1)
        return jnp.stack([one, total - one])
    tallies = jnp.asarray(split_up(number_of, total, most, lean), jnp.int32)
    couples = (number_of - 1) // 2
    giver, sink = tallies[1:1 + 2 * couples:2], tallies[2:2 + 2 * couples:2]
    margin = jnp.minimum(giver - 1, most - sink)
    shifted = jax.random.randint(jax.random.fold_in(key, 1), (couples,), 0, 1 << 20) % (margin + 1)
    tallies = tallies.at[1:1 + 2 * couples:2].set(giver - shifted).at[2:2 + 2 * couples:2].set(sink + shifted)
    return tallies[jax.random.permutation(jax.random.fold_in(key, 2), number_of)]


def bell_draw(rng, dims, deviation, reach, shards=(), kind=jnp.bfloat16):
    drawn = deviation * jax.random.normal(rng, dims, jnp.float32)
    if shards:
        drawn = drawn * block_levels(rng, dims, shards, -0.22, 0.18)
    return jnp.clip(drawn, -reach, reach).astype(kind)


def setup_inputs(seed: int = 0, part: int = 0) -> dict:
    seeds = jax.random.split(jax.random.key(seed), 9)
    own_keys = jax.random.split(jax.random.fold_in(seeds[8], part), 9)
    queries = draw_queries(jax.random.fold_in(jax.random.fold_in(seeds[8], part), 71), part)
    fresh_keys = bell_draw(own_keys[1], (TOKENS, HEADS * HEAD_DIM), 1.4, 8.375, ((0, 16),))
    fresh_values = bell_draw(own_keys[2], (TOKENS, HEADS * HEAD_DIM), 1.0, 6.0, ((0, 16),))
    cache_keys = draw_cache_keys(jax.random.fold_in(jax.random.fold_in(seeds[8], part), 71), part)
    cache_values = bell_draw(own_keys[4], (CACHE, HEADS * HEAD_DIM), 1.0, 6.0, ((0, 16),))
    lengths = uneven_parts(own_keys[5], BLOCKS, (3 * BLOCKS * TOK_DEV) // 5, TOK_DEV, 2).astype(jnp.int32)
    levels = plant(jax.random.randint(own_keys[6], (BLOCKS,), 0, LEVELS), jax.random.fold_in(own_keys[6], 1), 0, LEVELS - 1).astype(jnp.int32)
    gate_table = bell_draw(seeds[7], (LEVELS, HEADS * HEAD_DIM), 4.0, 24.0, (), jnp.float32)
    return dict(queries=queries, fresh_keys=fresh_keys, fresh_values=fresh_values, cache_keys=cache_keys, cache_values=cache_values, lengths=lengths, levels=levels, gate_table=gate_table)


def reference(queries, fresh_keys, fresh_values, cache_keys, cache_values, lengths, levels, gate_table):
    head_scale = 1.0 / math.sqrt(HEAD_DIM)
    feat_width = HEADS * HEAD_DIM
    query_blocks = queries.reshape(BLOCKS, TOK_DEV, HEADS, HEAD_DIM)
    padding = jnp.zeros((WIN - 1, TOK_DEV, HEADS, HEAD_DIM), fresh_keys.dtype)
    key_blocks = jnp.concatenate([padding, fresh_keys.reshape(BLOCKS, TOK_DEV, HEADS, HEAD_DIM)], 0)
    value_blocks = jnp.concatenate([padding, fresh_values.reshape(BLOCKS, TOK_DEV, HEADS, HEAD_DIM)], 0)
    length_padded = jnp.concatenate([jnp.zeros((WIN - 1,), jnp.int32), lengths.astype(jnp.int32)], 0)
    cache_key_heads = cache_keys.reshape(CACHE, HEADS, HEAD_DIM).astype(jnp.float32)
    cache_value_heads = cache_values.reshape(CACHE, HEADS, HEAD_DIM).astype(jnp.float32)
    slot_index = jnp.arange(TOK_DEV, dtype=jnp.int32)
    level_index = jnp.arange(LEVELS, dtype=jnp.int32)

    def one_block(block_index):
        query_block = lax.dynamic_index_in_dim(query_blocks, block_index, 0, keepdims=False).astype(jnp.float32)
        window_keys = lax.dynamic_slice_in_dim(key_blocks, block_index, WIN, 0)
        window_keys = window_keys.reshape(WIN * TOK_DEV, HEADS, HEAD_DIM).astype(jnp.float32)
        window_values = lax.dynamic_slice_in_dim(value_blocks, block_index, WIN, 0)
        window_values = window_values.reshape(WIN * TOK_DEV, HEADS, HEAD_DIM).astype(jnp.float32)
        window_lengths = lax.dynamic_slice_in_dim(length_padded, block_index, WIN, 0)
        live_mask = (slot_index[None, :] < window_lengths[:, None]).reshape(WIN * TOK_DEV)
        live_mask = jnp.concatenate([live_mask, jnp.ones((CACHE,), jnp.bool_)], 0)
        all_keys = jnp.concatenate([window_keys, cache_key_heads], 0)
        all_values = jnp.concatenate([window_values, cache_value_heads], 0)
        scores = jnp.einsum('thd,khd->htk', query_block, all_keys, precision=lax.Precision.HIGHEST) * head_scale
        scores = jnp.where(live_mask[None, None, :], scores, -jnp.inf)
        row_max = lax.optimization_barrier(jnp.max(scores, axis=2, keepdims=True))
        probabilities = jnp.exp(scores - row_max)
        denominator = lax.optimization_barrier(jnp.sum(probabilities, axis=2))
        rounded = lax.optimization_barrier(probabilities.astype(jnp.bfloat16)).astype(jnp.float32)
        attended = jnp.einsum('htk,khd->thd', rounded, all_values, precision=lax.Precision.HIGHEST)
        attended = attended / jnp.transpose(denominator)[:, :, None]
        block_level = lax.dynamic_index_in_dim(levels, block_index, 0, keepdims=False)
        onehot = (level_index == block_level).astype(jnp.float32)
        gate_row = jnp.dot(onehot[None, :], gate_table, precision=lax.Precision.HIGHEST)
        block_length = lax.dynamic_index_in_dim(lengths, block_index, 0, keepdims=False)
        modulated = attended.reshape(TOK_DEV, feat_width) * gate_row
        modulated = jnp.where((slot_index < block_length)[:, None], modulated, 0.0)
        return modulated.astype(jnp.bfloat16)
    outputs = lax.map(one_block, jnp.arange(BLOCKS, dtype=jnp.int32))
    return outputs.reshape(BLOCKS * TOK_DEV, feat_width)
```

```python
import math

import jax
import jax.numpy as jnp
from jax import lax
from jax.sharding import PartitionSpec as P

HEAD_DIM = 128
WIN = 4


def attend_block(carry_state, query_heads, key_block, value_block, live_mask):
    running_max, denominator, accumulated = carry_state
    head_count = query_heads.shape[1]
    head_depth = query_heads.shape[2]
    key_heads = key_block.reshape(key_block.shape[0], head_count, head_depth)
    value_heads = value_block.reshape(value_block.shape[0], head_count, head_depth)
    scores = jnp.einsum("thd,khd->htk", query_heads, key_heads, preferred_element_type=jnp.float32)
    scores = scores * (1.0 / math.sqrt(head_depth))
    scores = jnp.where(live_mask[None, None, :], scores, -jnp.inf)
    new_max = jnp.maximum(running_max, jnp.max(scores, axis=2))
    rescale = jnp.exp(running_max - new_max)
    probabilities = jnp.exp(scores - new_max[:, :, None])
    denominator = denominator * rescale + jnp.sum(probabilities, axis=2)
    weights = probabilities.astype(jnp.bfloat16)
    product = jnp.einsum("htk,khd->thd", weights, value_heads, preferred_element_type=jnp.float32)
    accumulated = accumulated * jnp.transpose(rescale)[:, :, None] + product
    return (new_max, denominator, accumulated)


def body(queries, fresh_keys, fresh_values, cache_keys, cache_values, lengths, levels, gate_table):
    row_count, feat_width = queries.shape
    head_depth = HEAD_DIM
    head_count = feat_width // head_depth
    size = lax.axis_size("group")
    me = lax.axis_index("group")
    query_heads = queries.reshape(row_count, head_count, head_depth)
    slot_index = jnp.arange(row_count, dtype=jnp.int32)

    cache_rows = cache_keys.shape[0]
    length_row = jnp.zeros((1, feat_width), jnp.bfloat16).at[0, 0].set(lengths[0].astype(jnp.bfloat16))
    packed = jnp.concatenate([cache_keys, cache_values, length_row], 0)
    gathered = lax.all_gather(packed, "group", axis=0, tiled=False)
    all_cache_keys = gathered[:, :cache_rows].reshape(-1, feat_width)
    all_cache_values = gathered[:, cache_rows:2 * cache_rows].reshape(-1, feat_width)
    all_lengths = gathered[:, 2 * cache_rows, 0].astype(jnp.int32)

    kv = jnp.stack([fresh_keys, fresh_values], 0)
    pairs_two = [(i, i + 2) for i in range(size - 2)]
    pairs_mixed = [(i, i + 1) for i in range(0, size - 1, 2)] + [(i, i + 3) for i in range(1, size - 3, 2)]
    from_two = lax.ppermute(kv, "group", pairs_two)
    from_mixed = lax.ppermute(kv, "group", pairs_mixed)
    pairs_swap = [(i, i ^ 1) for i in range(size)]
    from_swap = lax.ppermute(from_two, "group", pairs_swap)

    odd = (me % 2) == 1
    offset_mixed = jnp.where(odd, 1, 3)
    offset_swap = jnp.where(odd, 3, 1)

    def length_at(offset):
        source = me - offset
        return jnp.where(source >= 0, all_lengths[jnp.maximum(source, 0)], 0)

    block_lengths = jnp.stack([lengths[0], length_at(offset_mixed), length_at(2), length_at(offset_swap)])
    key_block = jnp.concatenate([fresh_keys, from_mixed[0], from_two[0], from_swap[0]], 0)
    value_block = jnp.concatenate([fresh_values, from_mixed[1], from_two[1], from_swap[1]], 0)
    live_mask = (slot_index[None, :] < block_lengths[:, None]).reshape(-1)

    initial = (
        jnp.full((head_count, row_count), -jnp.inf, jnp.float32),
        jnp.zeros((head_count, row_count), jnp.float32),
        jnp.zeros((row_count, head_count, head_depth), jnp.float32),
    )
    carry_state = attend_block(initial, query_heads, key_block, value_block, live_mask)
    cache_live = jnp.ones((all_cache_keys.shape[0],), jnp.bool_)
    final_state = attend_block(carry_state, query_heads, all_cache_keys, all_cache_values, cache_live)
    running_max, denominator, accumulated = final_state
    attended = (accumulated / jnp.transpose(denominator)[:, :, None]).reshape(row_count, feat_width)
    level_index = jnp.arange(gate_table.shape[0], dtype=jnp.int32)
    onehot = (level_index[None, :] == levels[:, None]).astype(jnp.float32)
    gate_row = jnp.dot(onehot, gate_table, precision=lax.Precision.HIGHEST)
    modulated = jnp.where((slot_index < lengths[0])[:, None], attended * gate_row, 0.0)
    return modulated.astype(jnp.bfloat16)


def solution(mesh):
    return jax.shard_map(
        body,
        mesh=mesh,
        in_specs=(
            P(("videos", "group"), None),
            P(("videos", "group"), None),
            P(("videos", "group"), None),
            P(("videos", "group"), None),
            P(("videos", "group"), None),
            P(("videos", "group")),
            P(("videos", "group")),
            P(),
        ),
        out_specs=P(("videos", "group"), None),
        check_vma=False,
    )
```

```python
import functools
import math

import jax
import jax.numpy as jnp
from jax import lax
from jax.experimental import pallas as pl
from jax.experimental.pallas import tpu as pltpu
from jax.sharding import PartitionSpec as P

HEAD_DIM = 128
WIN = 4
HEADS_PER_STEP = 4


def attention_kernel(table_ref, q_ref, k0, v0, k1, v1, k2, v2, k3, v3, ck, cv, gate_ref, o_ref, *, heads):
    scale = 1.0 / math.sqrt(HEAD_DIM)
    rows = q_ref.shape[0]
    slot = lax.broadcasted_iota(jnp.int32, (1, rows), 1)
    row = lax.broadcasted_iota(jnp.int32, (rows, 1), 0)
    level = table_ref[4]
    gate = gate_ref[pl.ds(level, 1), :]
    live_row = row < table_ref[0]
    blocks = ((k0, v0), (k1, v1), (k2, v2), (k3, v3))
    dims = (((1,), (1,)), ((), ()))
    for h in range(heads):
        cols = slice(h * HEAD_DIM, (h + 1) * HEAD_DIM)
        q = q_ref[:, cols]
        scores = []
        for j, (k_ref, _) in enumerate(blocks):
            s = lax.dot_general(q, k_ref[:, cols], dims, preferred_element_type=jnp.float32) * scale
            scores.append(jnp.where(slot < table_ref[j], s, -jnp.inf))
        scores.append(lax.dot_general(q, ck[:, cols], dims, preferred_element_type=jnp.float32) * scale)
        row_max = scores[0].max(axis=1, keepdims=True)
        for s in scores[1:]:
            row_max = jnp.maximum(row_max, s.max(axis=1, keepdims=True))
        values = [v_ref for _, v_ref in blocks] + [cv]
        denominator = jnp.zeros((rows, 1), jnp.float32)
        attended = jnp.zeros((rows, HEAD_DIM), jnp.float32)
        for s, v_ref in zip(scores, values):
            p = jnp.exp(s - row_max)
            denominator = denominator + p.sum(axis=1, keepdims=True)
            attended = attended + jnp.dot(p.astype(jnp.bfloat16), v_ref[:, cols], preferred_element_type=jnp.float32)
        attended = attended / denominator
        out = jnp.where(live_row, attended * gate[:, cols], 0.0)
        o_ref[:, cols] = out.astype(o_ref.dtype)


def attend(table, queries, kv_own, kv_a, kv_b, kv_c, cache_keys, cache_values, gate_table):
    rows, feat = queries.shape
    width = HEADS_PER_STEP * HEAD_DIM
    steps = feat // width
    cache_rows = cache_keys.shape[0]
    levels = gate_table.shape[0]
    row_block = pl.BlockSpec((rows, width), lambda h, t: (0, h))
    k_block = pl.BlockSpec((None, rows, width), lambda h, t: (0, 0, h))
    v_block = pl.BlockSpec((None, rows, width), lambda h, t: (1, 0, h))
    cache_block = pl.BlockSpec((cache_rows, width), lambda h, t: (0, h))
    gate_block = pl.BlockSpec((levels, width), lambda h, t: (0, h))
    grid_spec = pltpu.PrefetchScalarGridSpec(
        num_scalar_prefetch=1,
        grid=(steps,),
        in_specs=[row_block, k_block, v_block, k_block, v_block, k_block, v_block, k_block, v_block,
                  cache_block, cache_block, gate_block],
        out_specs=row_block,
    )
    keys = 4 * rows + cache_rows
    cost = pl.CostEstimate(
        flops=4 * rows * keys * feat,
        transcendentals=rows * keys * (feat // HEAD_DIM),
        bytes_accessed=2 * (2 * rows * feat + 8 * rows * feat + 2 * cache_rows * feat) + 4 * levels * feat,
    )
    return pl.pallas_call(
        functools.partial(attention_kernel, heads=HEADS_PER_STEP),
        out_shape=jax.ShapeDtypeStruct((rows, feat), jnp.bfloat16),
        grid_spec=grid_spec,
        cost_estimate=cost,
    )(table, queries, kv_own, kv_own, kv_a, kv_a, kv_b, kv_b, kv_c, kv_c, cache_keys, cache_values, gate_table)


def body(queries, fresh_keys, fresh_values, cache_keys, cache_values, lengths, levels, gate_table):
    row_count, feat_width = queries.shape
    size = lax.axis_size("group")
    me = lax.axis_index("group")

    cache_rows = cache_keys.shape[0]
    length_row = jnp.zeros((1, feat_width), jnp.bfloat16).at[0, 0].set(lengths[0].astype(jnp.bfloat16))
    packed = jnp.concatenate([cache_keys, cache_values, length_row], 0)
    gathered = lax.all_gather(packed, "group", axis=0, tiled=False)
    all_cache_keys = gathered[:, :cache_rows].reshape(-1, feat_width)
    all_cache_values = gathered[:, cache_rows:2 * cache_rows].reshape(-1, feat_width)
    all_lengths = gathered[:, 2 * cache_rows, 0].astype(jnp.int32)

    kv = jnp.stack([fresh_keys, fresh_values], 0)
    pairs_two = [(i, i + 2) for i in range(size - 2)]
    pairs_mixed = [(i, i + 1) for i in range(0, size - 1, 2)] + [(i, i + 3) for i in range(1, size - 3, 2)]
    from_two = lax.ppermute(kv, "group", pairs_two)
    from_mixed = lax.ppermute(kv, "group", pairs_mixed)
    pairs_swap = [(i, i ^ 1) for i in range(size)]
    from_swap = lax.ppermute(from_two, "group", pairs_swap)

    odd = (me % 2) == 1
    offset_mixed = jnp.where(odd, 1, 3)
    offset_swap = jnp.where(odd, 3, 1)

    def length_at(offset):
        source = me - offset
        return jnp.where(source >= 0, all_lengths[jnp.maximum(source, 0)], 0)

    table = jnp.stack([lengths[0], length_at(offset_mixed), length_at(2), length_at(offset_swap), levels[0]]).astype(jnp.int32)
    return attend(table, queries, kv, from_mixed, from_two, from_swap, all_cache_keys, all_cache_values, gate_table)


def solution(mesh):
    return jax.shard_map(
        body,
        mesh=mesh,
        in_specs=(
            P(("videos", "group"), None),
            P(("videos", "group"), None),
            P(("videos", "group"), None),
            P(("videos", "group"), None),
            P(("videos", "group"), None),
            P(("videos", "group")),
            P(("videos", "group")),
            P(),
        ),
        out_specs=P(("videos", "group"), None),
        check_vma=False,
    )
```

```python
import functools
import math

import jax
import jax.numpy as jnp
from jax import lax
from jax.experimental import pallas as pl
from jax.experimental.pallas import tpu as pltpu
from jax.sharding import PartitionSpec as P

HEAD_DIM = 128
WIN = 4
HEADS_PER_STEP = 4


def attention_kernel(table_ref, q_ref, k0, v0, k1, v1, k2, v2, k3, v3, ck, cv, gate_ref, o_ref, *, heads):
    scale = 1.0 / math.sqrt(HEAD_DIM)
    rows = q_ref.shape[0]
    slot = lax.broadcasted_iota(jnp.int32, (1, rows), 1)
    row = lax.broadcasted_iota(jnp.int32, (rows, 1), 0)
    level = table_ref[4]
    gate = gate_ref[pl.ds(level, 1), :]
    live_row = row < table_ref[0]
    blocks = ((k0, v0), (k1, v1), (k2, v2), (k3, v3))
    dims = (((1,), (1,)), ((), ()))
    for h in range(heads):
        cols = slice(h * HEAD_DIM, (h + 1) * HEAD_DIM)
        q = q_ref[:, cols]
        scores = []
        for j, (k_ref, _) in enumerate(blocks):
            s = lax.dot_general(q, k_ref[:, cols], dims, preferred_element_type=jnp.float32) * scale
            scores.append(jnp.where(slot < table_ref[j], s, -jnp.inf))
        scores.append(lax.dot_general(q, ck[:, cols], dims, preferred_element_type=jnp.float32) * scale)
        row_max = scores[0].max(axis=1, keepdims=True)
        for s in scores[1:]:
            row_max = jnp.maximum(row_max, s.max(axis=1, keepdims=True))
        values = [v_ref for _, v_ref in blocks] + [cv]
        denominator = jnp.zeros((rows, 1), jnp.float32)
        attended = jnp.zeros((rows, HEAD_DIM), jnp.float32)
        for s, v_ref in zip(scores, values):
            p = jnp.exp(s - row_max)
            denominator = denominator + p.sum(axis=1, keepdims=True)
            attended = attended + jnp.dot(p.astype(jnp.bfloat16), v_ref[:, cols], preferred_element_type=jnp.float32)
        attended = attended / denominator
        out = jnp.where(live_row, attended * gate[:, cols], 0.0)
        o_ref[:, cols] = out.astype(o_ref.dtype)


def attend(table, queries, kv_own, kv_a, kv_b, kv_c, cache_keys, cache_values, gate_table):
    rows, feat = queries.shape
    width = HEADS_PER_STEP * HEAD_DIM
    steps = feat // width
    cache_rows = cache_keys.shape[0]
    levels = gate_table.shape[0]
    row_block = pl.BlockSpec((rows, width), lambda h, t: (0, h))
    k_block = pl.BlockSpec((None, rows, width), lambda h, t: (0, 0, h))
    v_block = pl.BlockSpec((None, rows, width), lambda h, t: (1, 0, h))
    cache_block = pl.BlockSpec((cache_rows, width), lambda h, t: (0, h))
    gate_block = pl.BlockSpec((levels, width), lambda h, t: (0, h))
    grid_spec = pltpu.PrefetchScalarGridSpec(
        num_scalar_prefetch=1,
        grid=(steps,),
        in_specs=[row_block, k_block, v_block, k_block, v_block, k_block, v_block, k_block, v_block,
                  cache_block, cache_block, gate_block],
        out_specs=row_block,
    )
    keys = 4 * rows + cache_rows
    cost = pl.CostEstimate(
        flops=4 * rows * keys * feat,
        transcendentals=rows * keys * (feat // HEAD_DIM),
        bytes_accessed=2 * (2 * rows * feat + 8 * rows * feat + 2 * cache_rows * feat) + 4 * levels * feat,
    )
    return pl.pallas_call(
        functools.partial(attention_kernel, heads=HEADS_PER_STEP),
        out_shape=jax.ShapeDtypeStruct((rows, feat), jnp.bfloat16),
        grid_spec=grid_spec,
        cost_estimate=cost,
    )(table, queries, kv_own, kv_own, kv_a, kv_a, kv_b, kv_b, kv_c, kv_c, cache_keys, cache_values, gate_table)


def gather_pieces(piece, size):
    if size & (size - 1):
        return lax.all_gather(piece, "group", axis=0, tiled=False)
    me = lax.axis_index("group")
    held = piece[None]
    step = size // 2
    while step >= 1:
        other = lax.ppermute(held, "group", [(i, i ^ step) for i in range(size)])
        held = jnp.concatenate([held, other], 0)
        step //= 2
    return held


def body(queries, fresh_keys, fresh_values, cache_keys, cache_values, lengths, levels, gate_table):
    row_count, feat_width = queries.shape
    size = lax.axis_size("group")
    me = lax.axis_index("group")

    cache_rows = cache_keys.shape[0]
    tag_row = jnp.zeros((1, feat_width), jnp.bfloat16)
    tag_row = tag_row.at[0, 0].set(lengths[0].astype(jnp.bfloat16)).at[0, 1].set(me.astype(jnp.bfloat16))
    packed = jnp.concatenate([cache_keys, cache_values, tag_row], 0)
    gathered = gather_pieces(packed, size)
    all_cache_keys = gathered[:, :cache_rows].reshape(-1, feat_width)
    all_cache_values = gathered[:, cache_rows:2 * cache_rows].reshape(-1, feat_width)
    piece_lengths = gathered[:, 2 * cache_rows, 0].astype(jnp.int32)
    piece_index = gathered[:, 2 * cache_rows, 1].astype(jnp.int32)

    kv = jnp.stack([fresh_keys, fresh_values], 0)
    pairs_two = [(i, i + 2) for i in range(size - 2)]
    pairs_mixed = [(i, i + 1) for i in range(0, size - 1, 2)] + [(i, i + 3) for i in range(1, size - 3, 2)]
    from_two = lax.ppermute(kv, "group", pairs_two)
    from_mixed = lax.ppermute(kv, "group", pairs_mixed)
    pairs_swap = [(i, i ^ 1) for i in range(size)]
    from_swap = lax.ppermute(from_two, "group", pairs_swap)

    odd = (me % 2) == 1
    offset_mixed = jnp.where(odd, 1, 3)
    offset_swap = jnp.where(odd, 3, 1)

    def length_at(offset):
        source = me - offset
        return jnp.sum(jnp.where(piece_index == source, piece_lengths, 0))

    table = jnp.stack([lengths[0], length_at(offset_mixed), length_at(2), length_at(offset_swap), levels[0]]).astype(jnp.int32)
    return attend(table, queries, kv, from_mixed, from_two, from_swap, all_cache_keys, all_cache_values, gate_table)


def solution(mesh):
    return jax.shard_map(
        body,
        mesh=mesh,
        in_specs=(
            P(("videos", "group"), None),
            P(("videos", "group"), None),
            P(("videos", "group"), None),
            P(("videos", "group"), None),
            P(("videos", "group"), None),
            P(("videos", "group")),
            P(("videos", "group")),
            P(),
        ),
        out_specs=P(("videos", "group"), None),
        check_vma=False,
    )
```

```python
import functools
import math

import jax
import jax.numpy as jnp
from jax import lax
from jax.experimental import pallas as pl
from jax.experimental.pallas import tpu as pltpu
from jax.sharding import PartitionSpec as P

HEAD_DIM = 128
WIN = 4
HEADS_PER_STEP = 4


def attention_kernel(table_ref, q_ref, k0, v0, k1, v1, k2, v2, k3, v3, ck, cv, gate_ref, o_ref, *, heads):
    scale = 1.0 / math.sqrt(HEAD_DIM)
    rows = q_ref.shape[0]
    slot = lax.broadcasted_iota(jnp.int32, (1, rows), 1)
    row = lax.broadcasted_iota(jnp.int32, (rows, 1), 0)
    level = table_ref[4]
    gate = gate_ref[pl.ds(level, 1), :]
    live_row = row < table_ref[0]
    blocks = ((k0, v0), (k1, v1), (k2, v2), (k3, v3))
    dims = (((1,), (1,)), ((), ()))
    for h in range(heads):
        cols = slice(h * HEAD_DIM, (h + 1) * HEAD_DIM)
        q = q_ref[:, cols]
        scores = []
        for j, (k_ref, _) in enumerate(blocks):
            s = jnp.dot(q, k_ref[:, cols], preferred_element_type=jnp.float32) * scale
            scores.append(jnp.where(slot < table_ref[j], s, -jnp.inf))
        scores.append(lax.dot_general(q, ck[:, cols], dims, preferred_element_type=jnp.float32) * scale)
        row_max = scores[0].max(axis=1, keepdims=True)
        for s in scores[1:]:
            row_max = jnp.maximum(row_max, s.max(axis=1, keepdims=True))
        values = [v_ref for _, v_ref in blocks] + [cv]
        denominator = jnp.zeros((rows, 1), jnp.float32)
        attended = jnp.zeros((rows, HEAD_DIM), jnp.float32)
        for s, v_ref in zip(scores, values):
            p = jnp.exp(s - row_max)
            denominator = denominator + p.sum(axis=1, keepdims=True)
            attended = attended + jnp.dot(p.astype(jnp.bfloat16), v_ref[:, cols], preferred_element_type=jnp.float32)
        attended = attended / denominator
        out = jnp.where(live_row, attended * gate[:, cols], 0.0)
        o_ref[:, cols] = out.astype(o_ref.dtype)


def attend(table, queries, kv_own, kv_a, kv_b, kv_c, cache_keys, cache_values, gate_table):
    rows, feat = queries.shape
    width = HEADS_PER_STEP * HEAD_DIM
    steps = feat // width
    cache_rows = cache_keys.shape[0]
    levels = gate_table.shape[0]
    row_block = pl.BlockSpec((rows, width), lambda h, t: (0, h))
    k_block = pl.BlockSpec((None, rows, width), lambda h, t: (0, 0, h))
    v_block = pl.BlockSpec((None, rows, width), lambda h, t: (1, 0, h))
    cache_block = pl.BlockSpec((cache_rows, width), lambda h, t: (0, h))
    gate_block = pl.BlockSpec((levels, width), lambda h, t: (0, h))
    grid_spec = pltpu.PrefetchScalarGridSpec(
        num_scalar_prefetch=1,
        grid=(steps,),
        in_specs=[row_block, k_block, v_block, k_block, v_block, k_block, v_block, k_block, v_block,
                  cache_block, cache_block, gate_block],
        out_specs=row_block,
    )
    keys = 4 * rows + cache_rows
    cost = pl.CostEstimate(
        flops=4 * rows * keys * feat,
        transcendentals=rows * keys * (feat // HEAD_DIM),
        bytes_accessed=2 * (2 * rows * feat + 8 * rows * feat + 2 * cache_rows * feat) + 4 * levels * feat,
    )
    return pl.pallas_call(
        functools.partial(attention_kernel, heads=HEADS_PER_STEP),
        out_shape=jax.ShapeDtypeStruct((rows, feat), jnp.bfloat16),
        grid_spec=grid_spec,
        cost_estimate=cost,
    )(table, queries, kv_own, kv_own, kv_a, kv_a, kv_b, kv_b, kv_c, kv_c, cache_keys, cache_values, gate_table)


def gather_pieces(piece, size):
    if size & (size - 1):
        return lax.all_gather(piece, "group", axis=0, tiled=False)
    me = lax.axis_index("group")
    held = piece[None]
    step = size // 2
    while step >= 1:
        other = lax.ppermute(held, "group", [(i, i ^ step) for i in range(size)])
        held = jnp.concatenate([held, other], 0)
        step //= 2
    return held


def body(queries, fresh_keys, fresh_values, cache_keys, cache_values, lengths, levels, gate_table):
    row_count, feat_width = queries.shape
    size = lax.axis_size("group")
    me = lax.axis_index("group")

    cache_rows = cache_keys.shape[0]
    tag_row = jnp.zeros((1, feat_width), jnp.bfloat16)
    tag_row = tag_row.at[0, 0].set(lengths[0].astype(jnp.bfloat16)).at[0, 1].set(me.astype(jnp.bfloat16))
    packed = jnp.concatenate([cache_keys, cache_values, tag_row], 0)
    gathered = gather_pieces(packed, size)
    all_cache_keys = gathered[:, :cache_rows].reshape(-1, feat_width)
    all_cache_values = gathered[:, cache_rows:2 * cache_rows].reshape(-1, feat_width)
    piece_lengths = gathered[:, 2 * cache_rows, 0].astype(jnp.int32)
    piece_index = gathered[:, 2 * cache_rows, 1].astype(jnp.int32)

    head_count = feat_width // HEAD_DIM
    keys_by_head = fresh_keys.reshape(row_count, head_count, HEAD_DIM).transpose(2, 1, 0).reshape(HEAD_DIM, head_count * row_count)
    kv = jnp.stack([keys_by_head, fresh_values], 0)
    pairs_two = [(i, i + 2) for i in range(size - 2)]
    pairs_mixed = [(i, i + 1) for i in range(0, size - 1, 2)] + [(i, i + 3) for i in range(1, size - 3, 2)]
    from_two = lax.ppermute(kv, "group", pairs_two)
    from_mixed = lax.ppermute(kv, "group", pairs_mixed)
    pairs_swap = [(i, i ^ 1) for i in range(size)]
    from_swap = lax.ppermute(from_two, "group", pairs_swap)

    odd = (me % 2) == 1
    offsets = jnp.where(odd, jnp.array([1, 2, 3], jnp.int32), jnp.array([3, 2, 1], jnp.int32))
    sources = me - offsets
    previous = jnp.sum(jnp.where(piece_index[None, :] == sources[:, None], piece_lengths[None, :], 0), axis=1)
    table = jnp.concatenate([lengths[:1], previous, levels[:1]]).astype(jnp.int32)
    return attend(table, queries, kv, from_mixed, from_two, from_swap, all_cache_keys, all_cache_values, gate_table)


def solution(mesh):
    return jax.shard_map(
        body,
        mesh=mesh,
        in_specs=(
            P(("videos", "group"), None),
            P(("videos", "group"), None),
            P(("videos", "group"), None),
            P(("videos", "group"), None),
            P(("videos", "group"), None),
            P(("videos", "group")),
            P(("videos", "group")),
            P(),
        ),
        out_specs=P(("videos", "group"), None),
        check_vma=False,
    )
```

```python
import functools
import math

import jax
import jax.numpy as jnp
from jax import lax
from jax.experimental import pallas as pl
from jax.experimental.pallas import tpu as pltpu
from jax.sharding import PartitionSpec as P

HEAD_DIM = 128
WIN = 4
HEADS_PER_STEP = 4


def attention_kernel(table_ref, q_ref, k0, v0, k1, v1, k2, v2, k3, v3, ck, cv, gate_ref, o_ref, *, heads):
    scale = 1.0 / math.sqrt(HEAD_DIM)
    rows = q_ref.shape[0]
    slot = lax.broadcasted_iota(jnp.int32, (1, rows), 1)
    row = lax.broadcasted_iota(jnp.int32, (rows, 1), 0)
    level = table_ref[4]
    gate = gate_ref[pl.ds(level, 1), :]
    live_row = row < table_ref[0]
    blocks = ((k0, v0), (k1, v1), (k2, v2), (k3, v3))
    dims = (((1,), (1,)), ((), ()))
    for h in range(heads):
        cols = slice(h * HEAD_DIM, (h + 1) * HEAD_DIM)
        q = q_ref[:, cols]
        scores = []
        for j, (k_ref, _) in enumerate(blocks):
            s = jnp.dot(q, k_ref[:, cols], preferred_element_type=jnp.float32) * scale
            scores.append(jnp.where(slot < table_ref[j], s, -jnp.inf))
        scores.append(lax.dot_general(q, ck[:, cols], dims, preferred_element_type=jnp.float32) * scale)
        row_max = scores[0].max(axis=1, keepdims=True)
        for s in scores[1:]:
            row_max = jnp.maximum(row_max, s.max(axis=1, keepdims=True))
        values = [v_ref for _, v_ref in blocks] + [cv]
        denominator = jnp.zeros((rows, 1), jnp.float32)
        attended = jnp.zeros((rows, HEAD_DIM), jnp.float32)
        for s, v_ref in zip(scores, values):
            p = jnp.exp(s - row_max)
            denominator = denominator + p.sum(axis=1, keepdims=True)
            attended = attended + jnp.dot(p.astype(jnp.bfloat16), v_ref[:, cols], preferred_element_type=jnp.float32)
        attended = attended / denominator
        out = jnp.where(live_row, attended * gate[:, cols], 0.0)
        o_ref[:, cols] = out.astype(o_ref.dtype)


def attend(table, queries, kv_own, kv_a, kv_b, kv_c, cache, gate_table):
    rows, feat = queries.shape
    width = HEADS_PER_STEP * HEAD_DIM
    steps = feat // width
    cache_rows = cache.shape[0]
    levels = gate_table.shape[0]
    row_block = pl.BlockSpec((rows, width), lambda h, t: (0, h))
    k_block = pl.BlockSpec((None, rows, width), lambda h, t: (0, 0, h))
    v_block = pl.BlockSpec((None, rows, width), lambda h, t: (1, 0, h))
    cache_k_block = pl.BlockSpec((cache_rows, width), lambda h, t: (0, h))
    cache_v_block = pl.BlockSpec((cache_rows, width), lambda h, t: (0, steps + h))
    gate_block = pl.BlockSpec((levels, width), lambda h, t: (0, h))
    grid_spec = pltpu.PrefetchScalarGridSpec(
        num_scalar_prefetch=1,
        grid=(steps,),
        in_specs=[row_block, k_block, v_block, k_block, v_block, k_block, v_block, k_block, v_block,
                  cache_k_block, cache_v_block, gate_block],
        out_specs=row_block,
    )
    keys = 4 * rows + cache_rows
    cost = pl.CostEstimate(
        flops=4 * rows * keys * feat,
        transcendentals=rows * keys * (feat // HEAD_DIM),
        bytes_accessed=2 * (2 * rows * feat + 8 * rows * feat + 2 * cache_rows * feat) + 4 * levels * feat,
    )
    return pl.pallas_call(
        functools.partial(attention_kernel, heads=HEADS_PER_STEP),
        out_shape=jax.ShapeDtypeStruct((rows, feat), jnp.bfloat16),
        grid_spec=grid_spec,
        cost_estimate=cost,
    )(table, queries, kv_own, kv_own, kv_a, kv_a, kv_b, kv_b, kv_c, kv_c, cache, cache, gate_table)


def gather_pieces(piece, size):
    if size & (size - 1):
        return lax.all_gather(piece, "group", axis=0, tiled=True)
    held = piece
    step = size // 2
    while step >= 1:
        other = lax.ppermute(held, "group", [(i, i ^ step) for i in range(size)])
        held = jnp.concatenate([held, other], 0)
        step //= 2
    return held


def body(queries, fresh_keys, fresh_values, cache_keys, cache_values, lengths, levels, gate_table):
    row_count, feat_width = queries.shape
    size = lax.axis_size("group")
    me = lax.axis_index("group")

    cache_rows = cache_keys.shape[0]
    tag = jnp.zeros((cache_rows, HEAD_DIM), jnp.bfloat16)
    tag = tag.at[0, 0].set(lengths[0].astype(jnp.bfloat16)).at[0, 1].set(me.astype(jnp.bfloat16))
    packed = jnp.concatenate([cache_keys, cache_values, tag], 1)
    gathered = gather_pieces(packed, size)
    piece_lengths = gathered[:, 2 * feat_width].astype(jnp.int32)
    piece_index = gathered[:, 2 * feat_width + 1].astype(jnp.int32)

    head_count = feat_width // HEAD_DIM
    keys_by_head = fresh_keys.reshape(row_count, head_count, HEAD_DIM).transpose(2, 1, 0).reshape(HEAD_DIM, head_count * row_count)
    kv = jnp.stack([keys_by_head, fresh_values], 0)
    pairs_two = [(i, i + 2) for i in range(size - 2)]
    pairs_mixed = [(i, i + 1) for i in range(0, size - 1, 2)] + [(i, i + 3) for i in range(1, size - 3, 2)]
    from_two = lax.ppermute(kv, "group", pairs_two)
    from_mixed = lax.ppermute(kv, "group", pairs_mixed)
    pairs_swap = [(i, i ^ 1) for i in range(size)]
    from_swap = lax.ppermute(from_two, "group", pairs_swap)

    odd = (me % 2) == 1
    offsets = jnp.where(odd, jnp.array([1, 2, 3], jnp.int32), jnp.array([3, 2, 1], jnp.int32))
    sources = me - offsets
    previous = jnp.sum(jnp.where(piece_index[None, :] == sources[:, None], piece_lengths[None, :], 0), axis=1)
    table = jnp.concatenate([lengths[:1], previous, levels[:1]]).astype(jnp.int32)
    return attend(table, queries, kv, from_mixed, from_two, from_swap, gathered, gate_table)


def solution(mesh):
    return jax.shard_map(
        body,
        mesh=mesh,
        in_specs=(
            P(("videos", "group"), None),
            P(("videos", "group"), None),
            P(("videos", "group"), None),
            P(("videos", "group"), None),
            P(("videos", "group"), None),
            P(("videos", "group")),
            P(("videos", "group")),
            P(),
        ),
        out_specs=P(("videos", "group"), None),
        check_vma=False,
    )
```

```python
import functools
import math

import jax
import jax.numpy as jnp
from jax import lax
from jax.experimental import pallas as pl
from jax.experimental.pallas import tpu as pltpu
from jax.sharding import PartitionSpec as P

HEAD_DIM = 128
WIN = 4
HEADS_PER_STEP = 4


def attention_kernel(table_ref, q_ref, k0, v0, k1, v1, k2, v2, k3, v3, ck0, cv0, ck1, cv1, gate_ref, o_ref, *, heads):
    scale = 1.0 / math.sqrt(HEAD_DIM)
    rows = q_ref.shape[0]
    slot = lax.broadcasted_iota(jnp.int32, (1, rows), 1)
    row = lax.broadcasted_iota(jnp.int32, (rows, 1), 0)
    level = table_ref[4]
    gate = gate_ref[pl.ds(level, 1), :]
    live_row = row < table_ref[0]
    blocks = ((k0, v0), (k1, v1), (k2, v2), (k3, v3))
    dims = (((1,), (1,)), ((), ()))
    for h in range(heads):
        cols = slice(h * HEAD_DIM, (h + 1) * HEAD_DIM)
        q = q_ref[:, cols]
        scores = []
        for j, (k_ref, _) in enumerate(blocks):
            s = jnp.dot(q, k_ref[:, cols], preferred_element_type=jnp.float32) * scale
            scores.append(jnp.where(slot < table_ref[j], s, -jnp.inf))
        cache_keys = jnp.concatenate([ck0[:, cols], ck1[:, cols]], 0)
        scores.append(lax.dot_general(q, cache_keys, dims, preferred_element_type=jnp.float32) * scale)
        row_max = scores[0].max(axis=1, keepdims=True)
        for s in scores[1:]:
            row_max = jnp.maximum(row_max, s.max(axis=1, keepdims=True))
        values = [v_ref[:, cols] for _, v_ref in blocks] + [jnp.concatenate([cv0[:, cols], cv1[:, cols]], 0)]
        denominator = jnp.zeros((rows, 1), jnp.float32)
        attended = jnp.zeros((rows, HEAD_DIM), jnp.float32)
        for s, v_ref in zip(scores, values):
            p = jnp.exp(s - row_max)
            denominator = denominator + p.sum(axis=1, keepdims=True)
            attended = attended + jnp.dot(p.astype(jnp.bfloat16), v_ref, preferred_element_type=jnp.float32)
        attended = attended / denominator
        out = jnp.where(live_row, attended * gate[:, cols], 0.0)
        o_ref[:, cols] = out.astype(o_ref.dtype)


def attend(table, queries, kv_own, kv_a, kv_b, kv_c, cache_low, cache_high, gate_table):
    rows, feat = queries.shape
    width = HEADS_PER_STEP * HEAD_DIM
    steps = feat // width
    cache_rows = cache_low.shape[0]
    levels = gate_table.shape[0]
    row_block = pl.BlockSpec((rows, width), lambda h, t: (0, h))
    k_block = pl.BlockSpec((None, rows, width), lambda h, t: (0, 0, h))
    v_block = pl.BlockSpec((None, rows, width), lambda h, t: (1, 0, h))
    cache_k_block = pl.BlockSpec((cache_rows, width), lambda h, t: (0, h))
    cache_v_block = pl.BlockSpec((cache_rows, width), lambda h, t: (0, steps + h))
    gate_block = pl.BlockSpec((levels, width), lambda h, t: (0, h))
    grid_spec = pltpu.PrefetchScalarGridSpec(
        num_scalar_prefetch=1,
        grid=(steps,),
        in_specs=[row_block, k_block, v_block, k_block, v_block, k_block, v_block, k_block, v_block,
                  cache_k_block, cache_v_block, cache_k_block, cache_v_block, gate_block],
        out_specs=row_block,
    )
    keys = 4 * rows + 2 * cache_rows
    cost = pl.CostEstimate(
        flops=4 * rows * keys * feat,
        transcendentals=rows * keys * (feat // HEAD_DIM),
        bytes_accessed=2 * (2 * rows * feat + 8 * rows * feat + 4 * cache_rows * feat) + 4 * levels * feat,
    )
    return pl.pallas_call(
        functools.partial(attention_kernel, heads=HEADS_PER_STEP),
        out_shape=jax.ShapeDtypeStruct((rows, feat), jnp.bfloat16),
        grid_spec=grid_spec,
        cost_estimate=cost,
    )(table, queries, kv_own, kv_own, kv_a, kv_a, kv_b, kv_b, kv_c, kv_c, cache_low, cache_low, cache_high, cache_high, gate_table)


def gather_pieces(piece, size):
    if size & (size - 1) or size < 2:
        whole = lax.all_gather(piece, "group", axis=0, tiled=True)
        half = whole.shape[0] // 2
        return whole[:half], whole[half:]
    held = piece
    step = size // 2
    while step > 1:
        other = lax.ppermute(held, "group", [(i, i ^ step) for i in range(size)])
        held = jnp.concatenate([held, other], 0)
        step //= 2
    return held, lax.ppermute(held, "group", [(i, i ^ 1) for i in range(size)])


def body(queries, fresh_keys, fresh_values, cache_keys, cache_values, lengths, levels, gate_table):
    row_count, feat_width = queries.shape
    size = lax.axis_size("group")
    me = lax.axis_index("group")

    cache_rows = cache_keys.shape[0]
    tag = jnp.zeros((cache_rows, HEAD_DIM), jnp.bfloat16)
    tag = tag.at[0, 0].set(lengths[0].astype(jnp.bfloat16)).at[0, 1].set(me.astype(jnp.bfloat16))
    packed = jnp.concatenate([cache_keys, cache_values, tag], 1)
    gathered = None

    head_count = feat_width // HEAD_DIM
    keys_by_head = fresh_keys.reshape(row_count, head_count, HEAD_DIM).transpose(2, 1, 0).reshape(HEAD_DIM, head_count * row_count)
    kv = jnp.stack([keys_by_head, fresh_values], 0)
    pairs_two = [(i, i + 2) for i in range(size - 2)]
    pairs_mixed = [(i, i + 1) for i in range(0, size - 1, 2)] + [(i, i + 3) for i in range(1, size - 3, 2)]
    from_two = lax.ppermute(kv, "group", pairs_two)
    from_mixed = lax.ppermute(kv, "group", pairs_mixed)

    packed, from_mixed, from_two = lax.optimization_barrier((packed, from_mixed, from_two))
    pairs_swap = [(i, i ^ 1) for i in range(size)]
    from_swap = lax.ppermute(from_two, "group", pairs_swap)
    cache_low, cache_high = gather_pieces(packed, size)
    tags = jnp.concatenate([cache_low[:, 2 * feat_width:2 * feat_width + 2], cache_high[:, 2 * feat_width:2 * feat_width + 2]], 0)
    piece_lengths = tags[:, 0].astype(jnp.int32)
    piece_index = tags[:, 1].astype(jnp.int32)

    odd = (me % 2) == 1
    offsets = jnp.where(odd, jnp.array([1, 2, 3], jnp.int32), jnp.array([3, 2, 1], jnp.int32))
    sources = me - offsets
    previous = jnp.sum(jnp.where(piece_index[None, :] == sources[:, None], piece_lengths[None, :], 0), axis=1)
    table = jnp.concatenate([lengths[:1], previous, levels[:1]]).astype(jnp.int32)
    return attend(table, queries, kv, from_mixed, from_two, from_swap, cache_low, cache_high, gate_table)


def solution(mesh):
    return jax.shard_map(
        body,
        mesh=mesh,
        in_specs=(
            P(("videos", "group"), None),
            P(("videos", "group"), None),
            P(("videos", "group"), None),
            P(("videos", "group"), None),
            P(("videos", "group"), None),
            P(("videos", "group")),
            P(("videos", "group")),
            P(),
        ),
        out_specs=P(("videos", "group"), None),
        check_vma=False,
    )
```

```python
import functools
import math

import jax
import jax.numpy as jnp
from jax import lax
from jax.experimental import pallas as pl
from jax.experimental.pallas import tpu as pltpu
from jax.sharding import PartitionSpec as P

HEAD_DIM = 128
WIN = 4
HEADS_PER_STEP = 4


def attention_kernel(table_ref, q_ref, k0, v0, k1, v1, k2, v2, k3, v3, ck0, cv0, ck1, cv1, gate_ref, o_ref, *, heads):
    scale = 1.0 / math.sqrt(HEAD_DIM)
    rows = q_ref.shape[0]
    slot = lax.broadcasted_iota(jnp.int32, (1, rows), 1)
    row = lax.broadcasted_iota(jnp.int32, (rows, 1), 0)
    level = table_ref[4]
    gate = gate_ref[pl.ds(level, 1), :]
    live_row = row < table_ref[0]
    blocks = ((k0, v0), (k1, v1), (k2, v2), (k3, v3))
    dims = (((1,), (1,)), ((), ()))
    for h in range(heads):
        cols = slice(h * HEAD_DIM, (h + 1) * HEAD_DIM)
        q = q_ref[:, cols]
        scores = []
        for j, (k_ref, _) in enumerate(blocks):
            s = jnp.dot(q, k_ref[:, cols], preferred_element_type=jnp.float32) * scale
            scores.append(jnp.where(slot < table_ref[j], s, -jnp.inf))
        cache_keys = jnp.concatenate([ck0[:, cols], ck1[:, cols]], 0)
        scores.append(lax.dot_general(q, cache_keys, dims, preferred_element_type=jnp.float32) * scale)
        row_max = scores[0].max(axis=1, keepdims=True)
        for s in scores[1:]:
            row_max = jnp.maximum(row_max, s.max(axis=1, keepdims=True))
        values = [v_ref[:, cols] for _, v_ref in blocks] + [jnp.concatenate([cv0[:, cols], cv1[:, cols]], 0)]
        denominator = jnp.zeros((rows, 1), jnp.float32)
        attended = jnp.zeros((rows, HEAD_DIM), jnp.float32)
        for s, v_ref in zip(scores, values):
            p = jnp.exp(s - row_max)
            denominator = denominator + p.sum(axis=1, keepdims=True)
            attended = attended + jnp.dot(p.astype(jnp.bfloat16), v_ref, preferred_element_type=jnp.float32)
        attended = attended / denominator
        out = jnp.where(live_row, attended * gate[:, cols], 0.0)
        o_ref[:, cols] = out.astype(o_ref.dtype)


def attend(table, queries, kv_own, kv_a, kv_b, kv_c, cache_low, cache_high, gate_table):
    rows, feat = queries.shape
    width = HEADS_PER_STEP * HEAD_DIM
    steps = feat // width
    cache_rows = cache_low.shape[0]
    levels = gate_table.shape[0]
    row_block = pl.BlockSpec((rows, width), lambda h, t: (0, h))
    k_block = pl.BlockSpec((None, rows, width), lambda h, t: (0, 0, h))
    v_block = pl.BlockSpec((None, rows, width), lambda h, t: (1, 0, h))
    cache_k_block = pl.BlockSpec((cache_rows, width), lambda h, t: (0, h))
    cache_v_block = pl.BlockSpec((cache_rows, width), lambda h, t: (0, steps + h))
    gate_block = pl.BlockSpec((levels, width), lambda h, t: (0, h))
    grid_spec = pltpu.PrefetchScalarGridSpec(
        num_scalar_prefetch=1,
        grid=(steps,),
        in_specs=[row_block, k_block, v_block, k_block, v_block, k_block, v_block, k_block, v_block,
                  cache_k_block, cache_v_block, cache_k_block, cache_v_block, gate_block],
        out_specs=row_block,
    )
    keys = 4 * rows + 2 * cache_rows
    cost = pl.CostEstimate(
        flops=4 * rows * keys * feat,
        transcendentals=rows * keys * (feat // HEAD_DIM),
        bytes_accessed=2 * (2 * rows * feat + 8 * rows * feat + 4 * cache_rows * feat) + 4 * levels * feat,
    )
    return pl.pallas_call(
        functools.partial(attention_kernel, heads=HEADS_PER_STEP),
        out_shape=jax.ShapeDtypeStruct((rows, feat), jnp.bfloat16),
        grid_spec=grid_spec,
        cost_estimate=cost,
    )(table, queries, kv_own, kv_own, kv_a, kv_a, kv_b, kv_b, kv_c, kv_c, cache_low, cache_low, cache_high, cache_high, gate_table)


def gather_pieces(piece, size):
    if size & (size - 1) or size < 2:
        whole = lax.all_gather(piece, "group", axis=0, tiled=True)
        half = whole.shape[0] // 2
        return whole[:half], whole[half:]
    held = piece
    step = size // 2
    while step > 1:
        other = lax.ppermute(held, "group", [(i, i ^ step) for i in range(size)])
        held = jnp.concatenate([held, other], 0)
        step //= 2
    return held, lax.ppermute(held, "group", [(i, i ^ 1) for i in range(size)])


def body(queries, fresh_keys, fresh_values, cache_keys, cache_values, lengths, levels, gate_table):
    row_count, feat_width = queries.shape
    size = lax.axis_size("group")
    me = lax.axis_index("group")

    cache_rows = cache_keys.shape[0]
    tag = jnp.zeros((cache_rows, HEAD_DIM), jnp.bfloat16)
    tag = tag.at[0, 0].set(lengths[0].astype(jnp.bfloat16)).at[0, 1].set(me.astype(jnp.bfloat16))
    packed = jnp.concatenate([cache_keys, cache_values, tag], 1)
    gathered = None

    head_count = feat_width // HEAD_DIM
    keys_by_head = fresh_keys.reshape(row_count, head_count, HEAD_DIM).transpose(2, 1, 0).reshape(HEAD_DIM, head_count * row_count)
    kv = jnp.stack([keys_by_head, fresh_values], 0)
    pairs_two = [(i, i + 2) for i in range(size - 2)]
    pairs_mixed = [(i, i + 1) for i in range(0, size - 1, 2)] + [(i, i + 3) for i in range(1, size - 3, 2)]
    from_two = lax.ppermute(kv, "group", pairs_two)
    from_mixed = lax.ppermute(kv, "group", pairs_mixed)
    pairs_swap = [(i, i ^ 1) for i in range(size)]
    from_swap = lax.ppermute(from_two, "group", pairs_swap)

    cache_low, cache_high = lax.cond(me >= 0, lambda x: gather_pieces(x, size), lambda x: gather_pieces(x, size), packed)
    tags = jnp.concatenate([cache_low[:, 2 * feat_width:2 * feat_width + 2], cache_high[:, 2 * feat_width:2 * feat_width + 2]], 0)
    piece_lengths = tags[:, 0].astype(jnp.int32)
    piece_index = tags[:, 1].astype(jnp.int32)

    odd = (me % 2) == 1
    offsets = jnp.where(odd, jnp.array([1, 2, 3], jnp.int32), jnp.array([3, 2, 1], jnp.int32))
    sources = me - offsets
    previous = jnp.sum(jnp.where(piece_index[None, :] == sources[:, None], piece_lengths[None, :], 0), axis=1)
    table = jnp.concatenate([lengths[:1], previous, levels[:1]]).astype(jnp.int32)
    return attend(table, queries, kv, from_mixed, from_two, from_swap, cache_low, cache_high, gate_table)


def solution(mesh):
    return jax.shard_map(
        body,
        mesh=mesh,
        in_specs=(
            P(("videos", "group"), None),
            P(("videos", "group"), None),
            P(("videos", "group"), None),
            P(("videos", "group"), None),
            P(("videos", "group"), None),
            P(("videos", "group")),
            P(("videos", "group")),
            P(),
        ),
        out_specs=P(("videos", "group"), None),
        check_vma=False,
    )
```

```python
import functools
import math

import jax
import jax.numpy as jnp
from jax import lax
from jax.experimental import pallas as pl
from jax.experimental.pallas import tpu as pltpu
from jax.sharding import PartitionSpec as P

HEAD_DIM = 128
WIN = 4
HEADS_PER_STEP = 4


def attention_kernel(table_ref, q_ref, k0, v0, k1, v1, k2, v2, k3, v3, ck, cv, gate_ref, o_ref, *, heads):
    scale = 1.0 / math.sqrt(HEAD_DIM)
    rows = q_ref.shape[0]
    slot = lax.broadcasted_iota(jnp.int32, (1, rows), 1)
    row = lax.broadcasted_iota(jnp.int32, (rows, 1), 0)
    level = table_ref[4]
    gate = gate_ref[pl.ds(level, 1), :]
    live_row = row < table_ref[0]
    blocks = ((k0, v0), (k1, v1), (k2, v2), (k3, v3))
    dims = (((1,), (1,)), ((), ()))
    for h in range(heads):
        cols = slice(h * HEAD_DIM, (h + 1) * HEAD_DIM)
        q = q_ref[:, cols]
        scores = []
        for j, (k_ref, _) in enumerate(blocks):
            s = jnp.dot(q, k_ref[:, cols], preferred_element_type=jnp.float32) * scale
            scores.append(jnp.where(slot < table_ref[j], s, -jnp.inf))
        scores.append(lax.dot_general(q, ck[:, cols], dims, preferred_element_type=jnp.float32) * scale)
        row_max = scores[0].max(axis=1, keepdims=True)
        for s in scores[1:]:
            row_max = jnp.maximum(row_max, s.max(axis=1, keepdims=True))
        values = [v_ref for _, v_ref in blocks] + [cv]
        denominator = jnp.zeros((rows, 1), jnp.float32)
        attended = jnp.zeros((rows, HEAD_DIM), jnp.float32)
        for s, v_ref in zip(scores, values):
            p = jnp.exp(s - row_max)
            denominator = denominator + p.sum(axis=1, keepdims=True)
            attended = attended + jnp.dot(p.astype(jnp.bfloat16), v_ref[:, cols], preferred_element_type=jnp.float32)
        attended = attended / denominator
        out = jnp.where(live_row, attended * gate[:, cols], 0.0)
        o_ref[:, cols] = out.astype(o_ref.dtype)


def attend(table, queries, kv_own, kv_a, kv_b, kv_c, cache, gate_table):
    rows, feat = queries.shape
    width = HEADS_PER_STEP * HEAD_DIM
    steps = feat // width
    cache_rows = cache.shape[0]
    levels = gate_table.shape[0]
    row_block = pl.BlockSpec((rows, width), lambda h, t: (0, h))
    k_block = pl.BlockSpec((rows, width), lambda h, t: (0, h))
    v_block = pl.BlockSpec((rows, width), lambda h, t: (1, h))
    cache_k_block = pl.BlockSpec((cache_rows, width), lambda h, t: (0, h))
    cache_v_block = pl.BlockSpec((cache_rows, width), lambda h, t: (0, steps + h))
    gate_block = pl.BlockSpec((levels, width), lambda h, t: (0, h))
    grid_spec = pltpu.PrefetchScalarGridSpec(
        num_scalar_prefetch=1,
        grid=(steps,),
        in_specs=[row_block, k_block, v_block, k_block, v_block, k_block, v_block, k_block, v_block,
                  cache_k_block, cache_v_block, gate_block],
        out_specs=row_block,
    )
    keys = 4 * rows + cache_rows
    cost = pl.CostEstimate(
        flops=4 * rows * keys * feat,
        transcendentals=rows * keys * (feat // HEAD_DIM),
        bytes_accessed=2 * (2 * rows * feat + 8 * rows * feat + 2 * cache_rows * feat) + 4 * levels * feat,
    )
    return pl.pallas_call(
        functools.partial(attention_kernel, heads=HEADS_PER_STEP),
        out_shape=jax.ShapeDtypeStruct((rows, feat), jnp.bfloat16),
        grid_spec=grid_spec,
        cost_estimate=cost,
    )(table, queries, kv_own, kv_own, kv_a, kv_a, kv_b, kv_b, kv_c, kv_c, cache, cache, gate_table)


def shift_gather(held, size, shifts):
    for step in shifts:
        other = lax.ppermute(held, "group", [(i, (i + step) % size) for i in range(size)])
        held = jnp.concatenate([held, other], 0)
    return held


def keys_by_head_of(keys, rows, heads):
    return keys.reshape(rows, heads, HEAD_DIM).transpose(2, 1, 0).reshape(HEAD_DIM, heads * rows)


def body(queries, fresh_keys, fresh_values, cache_keys, cache_values, lengths, levels, gate_table):
    row_count, feat_width = queries.shape
    size = lax.axis_size("group")
    me = lax.axis_index("group")

    cache_rows = cache_keys.shape[0]
    tag = jnp.zeros((cache_rows, HEAD_DIM), jnp.bfloat16)
    tag = tag.at[0, 0].set(lengths[0].astype(jnp.bfloat16)).at[0, 1].set(me.astype(jnp.bfloat16))
    packed = jnp.concatenate([cache_keys, cache_values, tag], 1)
    head_count = feat_width // HEAD_DIM
    keys_by_head = keys_by_head_of(fresh_keys, row_count, head_count)
    piece_size = packed.size
    piece_rows = -(-piece_size // feat_width)
    piece_rows = -(-piece_rows // 8) * 8
    flat_piece = jnp.pad(packed.reshape(-1), (0, piece_rows * feat_width - piece_size)).reshape(piece_rows, feat_width)
    carrier = jnp.concatenate([keys_by_head, fresh_values, flat_piece], 0)
    pairs_two = [(i, (i + 2) % size) for i in range(size)]
    pairs_mixed = [(i, i + 1) for i in range(0, size - 1, 2)] + [(i, i + 3) for i in range(1, size - 3, 2)]
    from_two = lax.ppermute(carrier, "group", pairs_two)
    from_mixed = lax.ppermute(carrier, "group", pairs_mixed)
    from_two, from_mixed = lax.optimization_barrier((from_two, from_mixed))
    pairs_swap = [(i, i ^ 1) for i in range(size)]
    from_swap = lax.ppermute(from_two, "group", pairs_swap)

    piece_two = from_two[2 * row_count:].reshape(-1)[:piece_size].reshape(packed.shape)
    shifts = [1] + [1 << k for k in range(2, size.bit_length() - 1)]
    gathered = shift_gather(jnp.concatenate([packed, piece_two], 0), size, shifts)
    piece_lengths = gathered[:, 2 * feat_width].astype(jnp.int32)
    piece_index = gathered[:, 2 * feat_width + 1].astype(jnp.int32)

    odd = (me % 2) == 1
    offsets = jnp.where(odd, jnp.array([1, 2, 3], jnp.int32), jnp.array([3, 2, 1], jnp.int32))
    sources = me - offsets
    previous = jnp.sum(jnp.where(piece_index[None, :] == sources[:, None], piece_lengths[None, :], 0), axis=1)
    table = jnp.concatenate([lengths[:1], previous, levels[:1]]).astype(jnp.int32)
    return attend(table, queries, carrier, from_mixed, from_two, from_swap, gathered, gate_table)


def solution(mesh):
    return jax.shard_map(
        body,
        mesh=mesh,
        in_specs=(
            P(("videos", "group"), None),
            P(("videos", "group"), None),
            P(("videos", "group"), None),
            P(("videos", "group"), None),
            P(("videos", "group"), None),
            P(("videos", "group")),
            P(("videos", "group")),
            P(),
        ),
        out_specs=P(("videos", "group"), None),
        check_vma=False,
    )
```

```python
import functools
import math

import jax
import jax.numpy as jnp
from jax import lax
from jax.experimental import pallas as pl
from jax.experimental.pallas import tpu as pltpu
from jax.sharding import PartitionSpec as P

HEAD_DIM = 128
WIN = 4
HEADS_PER_STEP = 4


def attention_kernel(table_ref, q_ref, k0, v0, k1, v1, k2, v2, k3, v3, ck, cv, gate_ref, o_ref, *, heads):
    scale = 1.0 / math.sqrt(HEAD_DIM)
    rows = q_ref.shape[0]
    slot = lax.broadcasted_iota(jnp.int32, (1, rows), 1)
    row = lax.broadcasted_iota(jnp.int32, (rows, 1), 0)
    level = table_ref[4]
    gate = gate_ref[pl.ds(level, 1), :]
    live_row = row < table_ref[0]
    blocks = ((k0, v0), (k1, v1), (k2, v2), (k3, v3))
    dims = (((1,), (1,)), ((), ()))
    for h in range(heads):
        cols = slice(h * HEAD_DIM, (h + 1) * HEAD_DIM)
        q = q_ref[:, cols]
        scores = []
        for j, (k_ref, _) in enumerate(blocks):
            s = jnp.dot(q, k_ref[:, cols], preferred_element_type=jnp.float32) * scale
            scores.append(jnp.where(slot < table_ref[j], s, -jnp.inf))
        scores.append(lax.dot_general(q, ck[:, cols], dims, preferred_element_type=jnp.float32) * scale)
        row_max = scores[0].max(axis=1, keepdims=True)
        for s in scores[1:]:
            row_max = jnp.maximum(row_max, s.max(axis=1, keepdims=True))
        values = [v_ref for _, v_ref in blocks] + [cv]
        denominator = jnp.zeros((rows, 1), jnp.float32)
        attended = jnp.zeros((rows, HEAD_DIM), jnp.float32)
        for s, v_ref in zip(scores, values):
            p = jnp.exp(s - row_max)
            denominator = denominator + p.sum(axis=1, keepdims=True)
            attended = attended + jnp.dot(p.astype(jnp.bfloat16), v_ref[:, cols], preferred_element_type=jnp.float32)
        attended = attended / denominator
        out = jnp.where(live_row, attended * gate[:, cols], 0.0)
        o_ref[:, cols] = out.astype(o_ref.dtype)


def attend(table, queries, kv_own, kv_a, kv_b, kv_c, cache, gate_table):
    rows, feat = queries.shape
    width = HEADS_PER_STEP * HEAD_DIM
    steps = feat // width
    cache_rows = cache.shape[0]
    levels = gate_table.shape[0]
    row_block = pl.BlockSpec((rows, width), lambda h, t: (0, h))
    k_block = pl.BlockSpec((None, rows, width), lambda h, t: (0, 0, h))
    v_block = pl.BlockSpec((None, rows, width), lambda h, t: (1, 0, h))
    cache_k_block = pl.BlockSpec((cache_rows, width), lambda h, t: (0, h))
    cache_v_block = pl.BlockSpec((cache_rows, width), lambda h, t: (0, steps + h))
    gate_block = pl.BlockSpec((levels, width), lambda h, t: (0, h))
    grid_spec = pltpu.PrefetchScalarGridSpec(
        num_scalar_prefetch=1,
        grid=(steps,),
        in_specs=[row_block, k_block, v_block, k_block, v_block, k_block, v_block, k_block, v_block,
                  cache_k_block, cache_v_block, gate_block],
        out_specs=row_block,
    )
    keys = 4 * rows + cache_rows
    cost = pl.CostEstimate(
        flops=4 * rows * keys * feat,
        transcendentals=rows * keys * (feat // HEAD_DIM),
        bytes_accessed=2 * (2 * rows * feat + 8 * rows * feat + 2 * cache_rows * feat) + 4 * levels * feat,
    )
    return pl.pallas_call(
        functools.partial(attention_kernel, heads=HEADS_PER_STEP),
        out_shape=jax.ShapeDtypeStruct((rows, feat), jnp.bfloat16),
        grid_spec=grid_spec,
        cost_estimate=cost,
    )(table, queries, kv_own, kv_own, kv_a, kv_a, kv_b, kv_b, kv_c, kv_c, cache, cache, gate_table)


def gather_pieces(piece, size):
    if size & (size - 1):
        return lax.all_gather(piece, "group", axis=0, tiled=True)
    held = piece
    step = 1
    while step < size:
        other = lax.ppermute(held, "group", [(i, i ^ step) for i in range(size)])
        held = jnp.concatenate([held, other], 0)
        step *= 2
    return held


def body(queries, fresh_keys, fresh_values, cache_keys, cache_values, lengths, levels, gate_table):
    row_count, feat_width = queries.shape
    size = lax.axis_size("group")
    me = lax.axis_index("group")

    cache_rows = cache_keys.shape[0]
    tag = jnp.zeros((cache_rows, HEAD_DIM), jnp.bfloat16)
    tag = tag.at[0, 0].set(lengths[0].astype(jnp.bfloat16)).at[0, 1].set(me.astype(jnp.bfloat16))
    packed = jnp.concatenate([cache_keys, cache_values, tag], 1)
    gathered = gather_pieces(packed, size)
    piece_lengths = gathered[:, 2 * feat_width].astype(jnp.int32)
    piece_index = gathered[:, 2 * feat_width + 1].astype(jnp.int32)

    head_count = feat_width // HEAD_DIM
    keys_by_head = fresh_keys.reshape(row_count, head_count, HEAD_DIM).transpose(2, 1, 0).reshape(HEAD_DIM, head_count * row_count)
    kv = jnp.stack([keys_by_head, fresh_values], 0)
    pairs_two = [(i, i + 2) for i in range(size - 2)]
    pairs_mixed = [(i, i + 1) for i in range(0, size - 1, 2)] + [(i, i + 3) for i in range(1, size - 3, 2)]
    from_two = lax.ppermute(kv, "group", pairs_two)
    from_mixed = lax.ppermute(kv, "group", pairs_mixed)
    pairs_swap = [(i, i ^ 1) for i in range(size)]
    from_swap = lax.ppermute(from_two, "group", pairs_swap)

    odd = (me % 2) == 1
    offsets = jnp.where(odd, jnp.array([1, 2, 3], jnp.int32), jnp.array([3, 2, 1], jnp.int32))
    sources = me - offsets
    previous = jnp.sum(jnp.where(piece_index[None, :] == sources[:, None], piece_lengths[None, :], 0), axis=1)
    table = jnp.concatenate([lengths[:1], previous, levels[:1]]).astype(jnp.int32)
    return attend(table, queries, kv, from_mixed, from_two, from_swap, gathered, gate_table)


def solution(mesh):
    return jax.shard_map(
        body,
        mesh=mesh,
        in_specs=(
            P(("videos", "group"), None),
            P(("videos", "group"), None),
            P(("videos", "group"), None),
            P(("videos", "group"), None),
            P(("videos", "group"), None),
            P(("videos", "group")),
            P(("videos", "group")),
            P(),
        ),
        out_specs=P(("videos", "group"), None),
        check_vma=False,
    )
```

```python
import functools
import math

import jax
import jax.numpy as jnp
from jax import lax
from jax.experimental import pallas as pl
from jax.experimental.pallas import tpu as pltpu
from jax.sharding import PartitionSpec as P

HEAD_DIM = 128
WIN = 4
HEADS_PER_STEP = 4


def attention_kernel(table_ref, q_ref, k0, v0, k1, v1, k2, v2, k3, v3, ck, cv, gate_ref, o_ref, *, heads):
    scale = 1.0 / math.sqrt(HEAD_DIM)
    rows = q_ref.shape[0]
    slot = lax.broadcasted_iota(jnp.int32, (1, rows), 1)
    row = lax.broadcasted_iota(jnp.int32, (rows, 1), 0)
    level = table_ref[4]
    gate = gate_ref[pl.ds(level, 1), :]
    live_row = row < table_ref[0]
    blocks = ((k0, v0), (k1, v1), (k2, v2), (k3, v3))
    dims = (((1,), (1,)), ((), ()))
    for h in range(heads):
        cols = slice(h * HEAD_DIM, (h + 1) * HEAD_DIM)
        q = q_ref[:, cols]
        scores = []
        for j, (k_ref, _) in enumerate(blocks):
            s = jnp.dot(q, k_ref[:, cols], preferred_element_type=jnp.float32) * scale
            scores.append(jnp.where(slot < table_ref[j], s, -jnp.inf))
        scores.append(lax.dot_general(q, ck[:, cols], dims, preferred_element_type=jnp.float32) * scale)
        row_max = scores[0].max(axis=1, keepdims=True)
        for s in scores[1:]:
            row_max = jnp.maximum(row_max, s.max(axis=1, keepdims=True))
        values = [v_ref for _, v_ref in blocks] + [cv]
        denominator = jnp.zeros((rows, 1), jnp.float32)
        attended = jnp.zeros((rows, HEAD_DIM), jnp.float32)
        for s, v_ref in zip(scores, values):
            p = jnp.exp(s - row_max)
            denominator = denominator + p.sum(axis=1, keepdims=True)
            attended = attended + jnp.dot(p.astype(jnp.bfloat16), v_ref[:, cols], preferred_element_type=jnp.float32)
        attended = attended / denominator
        out = jnp.where(live_row, attended * gate[:, cols], 0.0)
        o_ref[:, cols] = out.astype(o_ref.dtype)


def attend(table, queries, kv_own, kv_a, kv_b, kv_c, cache, gate_table):
    rows, feat = queries.shape
    width = HEADS_PER_STEP * HEAD_DIM
    steps = feat // width
    cache_rows = cache.shape[0]
    levels = gate_table.shape[0]
    row_block = pl.BlockSpec((rows, width), lambda h, t: (0, h))
    k_block = pl.BlockSpec((None, rows, width), lambda h, t: (0, 0, h))
    v_block = pl.BlockSpec((None, rows, width), lambda h, t: (1, 0, h))
    cache_k_block = pl.BlockSpec((cache_rows, width), lambda h, t: (0, h))
    cache_v_block = pl.BlockSpec((cache_rows, width), lambda h, t: (0, steps + h))
    gate_block = pl.BlockSpec((levels, width), lambda h, t: (0, h))
    grid_spec = pltpu.PrefetchScalarGridSpec(
        num_scalar_prefetch=1,
        grid=(steps,),
        in_specs=[row_block, k_block, v_block, k_block, v_block, k_block, v_block, k_block, v_block,
                  cache_k_block, cache_v_block, gate_block],
        out_specs=row_block,
    )
    keys = 4 * rows + cache_rows
    cost = pl.CostEstimate(
        flops=4 * rows * keys * feat,
        transcendentals=rows * keys * (feat // HEAD_DIM),
        bytes_accessed=2 * (2 * rows * feat + 8 * rows * feat + 2 * cache_rows * feat) + 4 * levels * feat,
    )
    return pl.pallas_call(
        functools.partial(attention_kernel, heads=HEADS_PER_STEP),
        out_shape=jax.ShapeDtypeStruct((rows, feat), jnp.bfloat16),
        grid_spec=grid_spec,
        cost_estimate=cost,
    )(table, queries, kv_own, kv_own, kv_a, kv_a, kv_b, kv_b, kv_c, kv_c, cache, cache, gate_table)


def gather_pieces(piece, size):
    if size & (size - 1):
        return lax.all_gather(piece, "group", axis=0, tiled=True)
    held = piece
    steps = [1] + [size >> k for k in range(1, size.bit_length() - 1)]
    for step in steps:
        other = lax.ppermute(held, "group", [(i, i ^ step) for i in range(size)])
        held = jnp.concatenate([held, other], 0)
    return held


def body(queries, fresh_keys, fresh_values, cache_keys, cache_values, lengths, levels, gate_table):
    row_count, feat_width = queries.shape
    size = lax.axis_size("group")
    me = lax.axis_index("group")

    cache_rows = cache_keys.shape[0]
    tag = jnp.zeros((cache_rows, HEAD_DIM), jnp.bfloat16)
    tag = tag.at[0, 0].set(lengths[0].astype(jnp.bfloat16)).at[0, 1].set(me.astype(jnp.bfloat16))
    packed = jnp.concatenate([cache_keys, cache_values, tag], 1)
    gathered = gather_pieces(packed, size)
    piece_lengths = gathered[:, 2 * feat_width].astype(jnp.int32)
    piece_index = gathered[:, 2 * feat_width + 1].astype(jnp.int32)

    head_count = feat_width // HEAD_DIM
    keys_by_head = fresh_keys.reshape(row_count, head_count, HEAD_DIM).transpose(2, 1, 0).reshape(HEAD_DIM, head_count * row_count)
    kv = jnp.stack([keys_by_head, fresh_values], 0)
    pairs_two = [(i, i + 2) for i in range(size - 2)]
    pairs_mixed = [(i, i + 1) for i in range(0, size - 1, 2)] + [(i, i + 3) for i in range(1, size - 3, 2)]
    from_two = lax.ppermute(kv, "group", pairs_two)
    from_mixed = lax.ppermute(kv, "group", pairs_mixed)
    pairs_swap = [(i, i ^ 1) for i in range(size)]
    from_swap = lax.ppermute(from_two, "group", pairs_swap)

    odd = (me % 2) == 1
    offsets = jnp.where(odd, jnp.array([1, 2, 3], jnp.int32), jnp.array([3, 2, 1], jnp.int32))
    sources = me - offsets
    previous = jnp.sum(jnp.where(piece_index[None, :] == sources[:, None], piece_lengths[None, :], 0), axis=1)
    table = jnp.concatenate([lengths[:1], previous, levels[:1]]).astype(jnp.int32)
    return attend(table, queries, kv, from_mixed, from_two, from_swap, gathered, gate_table)


def solution(mesh):
    return jax.shard_map(
        body,
        mesh=mesh,
        in_specs=(
            P(("videos", "group"), None),
            P(("videos", "group"), None),
            P(("videos", "group"), None),
            P(("videos", "group"), None),
            P(("videos", "group"), None),
            P(("videos", "group")),
            P(("videos", "group")),
            P(),
        ),
        out_specs=P(("videos", "group"), None),
        check_vma=False,
    )
```

```python
import functools
import math

import jax
import jax.numpy as jnp
from jax import lax
from jax.experimental import pallas as pl
from jax.experimental.pallas import tpu as pltpu
from jax.sharding import PartitionSpec as P

HEAD_DIM = 128
WIN = 4
HEADS_PER_STEP = 8


def attention_kernel(table_ref, q_ref, k0, v0, k1, v1, k2, v2, k3, v3, ck, cv, gate_ref, o_ref, *, heads):
    scale = 1.0 / math.sqrt(HEAD_DIM)
    rows = q_ref.shape[0]
    slot = lax.broadcasted_iota(jnp.int32, (1, rows), 1)
    row = lax.broadcasted_iota(jnp.int32, (rows, 1), 0)
    level = table_ref[4]
    gate = gate_ref[pl.ds(level, 1), :]
    live_row = row < table_ref[0]
    blocks = ((k0, v0), (k1, v1), (k2, v2), (k3, v3))
    dims = (((1,), (1,)), ((), ()))
    for h in range(heads):
        cols = slice(h * HEAD_DIM, (h + 1) * HEAD_DIM)
        q = q_ref[:, cols]
        scores = []
        for j, (k_ref, _) in enumerate(blocks):
            s = jnp.dot(q, k_ref[:, cols], preferred_element_type=jnp.float32) * scale
            scores.append(jnp.where(slot < table_ref[j], s, -jnp.inf))
        scores.append(lax.dot_general(q, ck[:, cols], dims, preferred_element_type=jnp.float32) * scale)
        row_max = scores[0].max(axis=1, keepdims=True)
        for s in scores[1:]:
            row_max = jnp.maximum(row_max, s.max(axis=1, keepdims=True))
        values = [v_ref for _, v_ref in blocks] + [cv]
        denominator = jnp.zeros((rows, 1), jnp.float32)
        attended = jnp.zeros((rows, HEAD_DIM), jnp.float32)
        for s, v_ref in zip(scores, values):
            p = jnp.exp(s - row_max)
            denominator = denominator + p.sum(axis=1, keepdims=True)
            attended = attended + jnp.dot(p.astype(jnp.bfloat16), v_ref[:, cols], preferred_element_type=jnp.float32)
        attended = attended / denominator
        out = jnp.where(live_row, attended * gate[:, cols], 0.0)
        o_ref[:, cols] = out.astype(o_ref.dtype)


def attend(table, queries, kv_own, kv_a, kv_b, kv_c, cache, gate_table):
    rows, feat = queries.shape
    width = HEADS_PER_STEP * HEAD_DIM
    steps = feat // width
    cache_rows = cache.shape[0]
    levels = gate_table.shape[0]
    row_block = pl.BlockSpec((rows, width), lambda h, t: (0, h))
    k_block = pl.BlockSpec((None, rows, width), lambda h, t: (0, 0, h))
    v_block = pl.BlockSpec((None, rows, width), lambda h, t: (1, 0, h))
    cache_k_block = pl.BlockSpec((cache_rows, width), lambda h, t: (0, h))
    cache_v_block = pl.BlockSpec((cache_rows, width), lambda h, t: (0, steps + h))
    gate_block = pl.BlockSpec((levels, width), lambda h, t: (0, h))
    grid_spec = pltpu.PrefetchScalarGridSpec(
        num_scalar_prefetch=1,
        grid=(steps,),
        in_specs=[row_block, k_block, v_block, k_block, v_block, k_block, v_block, k_block, v_block,
                  cache_k_block, cache_v_block, gate_block],
        out_specs=row_block,
    )
    keys = 4 * rows + cache_rows
    cost = pl.CostEstimate(
        flops=4 * rows * keys * feat,
        transcendentals=rows * keys * (feat // HEAD_DIM),
        bytes_accessed=2 * (2 * rows * feat + 8 * rows * feat + 2 * cache_rows * feat) + 4 * levels * feat,
    )
    return pl.pallas_call(
        functools.partial(attention_kernel, heads=HEADS_PER_STEP),
        out_shape=jax.ShapeDtypeStruct((rows, feat), jnp.bfloat16),
        grid_spec=grid_spec,
        cost_estimate=cost,
    )(table, queries, kv_own, kv_own, kv_a, kv_a, kv_b, kv_b, kv_c, kv_c, cache, cache, gate_table)


def gather_pieces(piece, size):
    if size & (size - 1):
        return lax.all_gather(piece, "group", axis=0, tiled=True)
    held = piece
    step = size // 2
    while step >= 1:
        other = lax.ppermute(held, "group", [(i, i ^ step) for i in range(size)])
        held = jnp.concatenate([held, other], 0)
        step //= 2
    return held


def body(queries, fresh_keys, fresh_values, cache_keys, cache_values, lengths, levels, gate_table):
    row_count, feat_width = queries.shape
    size = lax.axis_size("group")
    me = lax.axis_index("group")

    cache_rows = cache_keys.shape[0]
    tag = jnp.zeros((cache_rows, HEAD_DIM), jnp.bfloat16)
    tag = tag.at[0, 0].set(lengths[0].astype(jnp.bfloat16)).at[0, 1].set(me.astype(jnp.bfloat16))
    packed = jnp.concatenate([cache_keys, cache_values, tag], 1)
    gathered = gather_pieces(packed, size)
    piece_lengths = gathered[:, 2 * feat_width].astype(jnp.int32)
    piece_index = gathered[:, 2 * feat_width + 1].astype(jnp.int32)

    head_count = feat_width // HEAD_DIM
    keys_by_head = fresh_keys.reshape(row_count, head_count, HEAD_DIM).transpose(2, 1, 0).reshape(HEAD_DIM, head_count * row_count)
    kv = jnp.stack([keys_by_head, fresh_values], 0)
    pairs_two = [(i, i + 2) for i in range(size - 2)]
    pairs_mixed = [(i, i + 1) for i in range(0, size - 1, 2)] + [(i, i + 3) for i in range(1, size - 3, 2)]
    from_two = lax.ppermute(kv, "group", pairs_two)
    from_mixed = lax.ppermute(kv, "group", pairs_mixed)
    pairs_swap = [(i, i ^ 1) for i in range(size)]
    from_swap = lax.ppermute(from_two, "group", pairs_swap)

    odd = (me % 2) == 1
    offsets = jnp.where(odd, jnp.array([1, 2, 3], jnp.int32), jnp.array([3, 2, 1], jnp.int32))
    sources = me - offsets
    previous = jnp.sum(jnp.where(piece_index[None, :] == sources[:, None], piece_lengths[None, :], 0), axis=1)
    table = jnp.concatenate([lengths[:1], previous, levels[:1]]).astype(jnp.int32)
    return attend(table, queries, kv, from_mixed, from_two, from_swap, gathered, gate_table)


def solution(mesh):
    return jax.shard_map(
        body,
        mesh=mesh,
        in_specs=(
            P(("videos", "group"), None),
            P(("videos", "group"), None),
            P(("videos", "group"), None),
            P(("videos", "group"), None),
            P(("videos", "group"), None),
            P(("videos", "group")),
            P(("videos", "group")),
            P(),
        ),
        out_specs=P(("videos", "group"), None),
        check_vma=False,
    )
```

```python
import functools
import math

import jax
import jax.numpy as jnp
from jax import lax
from jax.experimental import pallas as pl
from jax.experimental.pallas import tpu as pltpu
from jax.sharding import PartitionSpec as P

HEAD_DIM = 128
WIN = 4
HEADS_PER_STEP = 8


def partial_kernel(table_ref, q_ref, k0, v0, k2, v2, k3, v3, ck, cv, m_ref, l_ref, acc_ref, *, heads):
    scale = 1.0 / math.sqrt(HEAD_DIM)
    rows = q_ref.shape[0]
    slot = lax.broadcasted_iota(jnp.int32, (1, rows), 1)
    dims = (((1,), (1,)), ((), ()))
    blocks = ((k0, v0, 0), (k2, v2, 2), (k3, v3, 3))
    for h in range(heads):
        cols = slice(h * HEAD_DIM, (h + 1) * HEAD_DIM)
        q = q_ref[:, cols]
        scores = []
        for k_ref, _, j in blocks:
            s = jnp.dot(q, k_ref[:, cols], preferred_element_type=jnp.float32) * scale
            scores.append(jnp.where(slot < table_ref[j], s, -jnp.inf))
        scores.append(lax.dot_general(q, ck[:, cols], dims, preferred_element_type=jnp.float32) * scale)
        window = jnp.maximum(jnp.maximum(scores[0], scores[1]), scores[2])
        row_max = jnp.maximum(window.max(axis=1, keepdims=True), scores[3].max(axis=1, keepdims=True))
        values = [v_ref[:, cols] for _, v_ref, _ in blocks] + [cv[:, cols]]
        probabilities = [jnp.exp(s - row_max) for s in scores]
        window_sum = (probabilities[0] + probabilities[1]) + probabilities[2]
        denominator = window_sum.sum(axis=1, keepdims=True) + probabilities[3].sum(axis=1, keepdims=True)
        attended = jnp.zeros((rows, HEAD_DIM), jnp.float32)
        for p, v in zip(probabilities, values):
            attended = attended + jnp.dot(p.astype(jnp.bfloat16), v, preferred_element_type=jnp.float32)
        m_ref[:, h:h + 1] = row_max
        l_ref[:, h:h + 1] = denominator
        acc_ref[:, cols] = attended


def finish_kernel(table_ref, q_ref, k1, v1, m_ref, l_ref, acc_ref, gate_ref, o_ref, *, heads):
    scale = 1.0 / math.sqrt(HEAD_DIM)
    rows = q_ref.shape[0]
    slot = lax.broadcasted_iota(jnp.int32, (1, rows), 1)
    row = lax.broadcasted_iota(jnp.int32, (rows, 1), 0)
    gate = gate_ref[pl.ds(table_ref[4], 1), :]
    live_row = row < table_ref[0]
    for h in range(heads):
        cols = slice(h * HEAD_DIM, (h + 1) * HEAD_DIM)
        s = jnp.dot(q_ref[:, cols], k1[:, cols], preferred_element_type=jnp.float32) * scale
        s = jnp.where(slot < table_ref[1], s, -jnp.inf)
        old_max = m_ref[:, h:h + 1]
        new_max = jnp.maximum(old_max, s.max(axis=1, keepdims=True))
        rescale = jnp.exp(old_max - new_max)
        p = jnp.exp(s - new_max)
        denominator = l_ref[:, h:h + 1] * rescale + p.sum(axis=1, keepdims=True)
        attended = acc_ref[:, cols] * rescale + jnp.dot(p.astype(jnp.bfloat16), v1[:, cols], preferred_element_type=jnp.float32)
        attended = attended / denominator
        o_ref[:, cols] = jnp.where(live_row, attended * gate[:, cols], 0.0).astype(o_ref.dtype)


def attend(table, queries, kv_own, kv_a, kv_b, kv_c, cache, gate_table):
    rows, feat = queries.shape
    width = HEADS_PER_STEP * HEAD_DIM
    steps = feat // width
    cache_rows = cache.shape[0]
    levels = gate_table.shape[0]
    row_block = pl.BlockSpec((rows, width), lambda h, t: (0, h))
    k_block = pl.BlockSpec((None, rows, width), lambda h, t: (0, 0, h))
    v_block = pl.BlockSpec((None, rows, width), lambda h, t: (1, 0, h))
    cache_k_block = pl.BlockSpec((cache_rows, width), lambda h, t: (0, h))
    cache_v_block = pl.BlockSpec((cache_rows, width), lambda h, t: (0, steps + h))
    gate_block = pl.BlockSpec((levels, width), lambda h, t: (0, h))
    stat_block = pl.BlockSpec((None, rows, HEADS_PER_STEP), lambda h, t: (h, 0, 0))
    stat_shape = jax.ShapeDtypeStruct((steps, rows, HEADS_PER_STEP), jnp.float32)
    keys = 3 * rows + cache_rows
    m, l, acc = pl.pallas_call(
        functools.partial(partial_kernel, heads=HEADS_PER_STEP),
        out_shape=(stat_shape, stat_shape, jax.ShapeDtypeStruct((rows, feat), jnp.float32)),
        grid_spec=pltpu.PrefetchScalarGridSpec(
            num_scalar_prefetch=1,
            grid=(steps,),
            in_specs=[row_block, k_block, v_block, k_block, v_block, k_block, v_block, cache_k_block, cache_v_block],
            out_specs=(stat_block, stat_block, row_block),
        ),
        cost_estimate=pl.CostEstimate(
            flops=4 * rows * keys * feat,
            transcendentals=rows * keys * (feat // HEAD_DIM),
            bytes_accessed=2 * (7 * rows * feat + 2 * cache_rows * feat) + 4 * rows * feat,
        ),
    )(table, queries, kv_own, kv_own, kv_b, kv_b, kv_c, kv_c, cache, cache)
    return pl.pallas_call(
        functools.partial(finish_kernel, heads=HEADS_PER_STEP),
        out_shape=jax.ShapeDtypeStruct((rows, feat), jnp.bfloat16),
        grid_spec=pltpu.PrefetchScalarGridSpec(
            num_scalar_prefetch=1,
            grid=(steps,),
            in_specs=[row_block, k_block, v_block, stat_block, stat_block, row_block, gate_block],
            out_specs=row_block,
        ),
        cost_estimate=pl.CostEstimate(
            flops=4 * rows * rows * feat,
            transcendentals=rows * rows * (feat // HEAD_DIM),
            bytes_accessed=2 * (4 * rows * feat) + 4 * rows * feat + 4 * levels * feat,
        ),
    )(table, queries, kv_a, kv_a, m, l, acc, gate_table)


def gather_pieces(piece, size):
    if size & (size - 1):
        return lax.all_gather(piece, "group", axis=0, tiled=True)
    held = piece
    step = size // 2
    while step >= 1:
        other = lax.ppermute(held, "group", [(i, i ^ step) for i in range(size)])
        held = jnp.concatenate([held, other], 0)
        step //= 2
    return held


def body(queries, fresh_keys, fresh_values, cache_keys, cache_values, lengths, levels, gate_table):
    row_count, feat_width = queries.shape
    size = lax.axis_size("group")
    me = lax.axis_index("group")

    cache_rows = cache_keys.shape[0]
    tag = jnp.zeros((cache_rows, HEAD_DIM), jnp.bfloat16)
    tag = tag.at[0, 0].set(lengths[0].astype(jnp.bfloat16)).at[0, 1].set(me.astype(jnp.bfloat16))
    packed = jnp.concatenate([cache_keys, cache_values, tag], 1)
    gathered = gather_pieces(packed, size)
    piece_lengths = gathered[:, 2 * feat_width].astype(jnp.int32)
    piece_index = gathered[:, 2 * feat_width + 1].astype(jnp.int32)

    head_count = feat_width // HEAD_DIM
    keys_by_head = fresh_keys.reshape(row_count, head_count, HEAD_DIM).transpose(2, 1, 0).reshape(HEAD_DIM, head_count * row_count)
    kv = jnp.stack([keys_by_head, fresh_values], 0)
    pairs_two = [(i, i + 2) for i in range(size - 2)]
    pairs_mixed = [(i, i + 1) for i in range(0, size - 1, 2)] + [(i, i + 3) for i in range(1, size - 3, 2)]
    from_two = lax.ppermute(kv, "group", pairs_two)
    from_mixed = lax.ppermute(kv, "group", pairs_mixed)
    pairs_swap = [(i, i ^ 1) for i in range(size)]
    from_swap = lax.ppermute(from_two, "group", pairs_swap)

    odd = (me % 2) == 1
    offsets = jnp.where(odd, jnp.array([1, 2, 3], jnp.int32), jnp.array([3, 2, 1], jnp.int32))
    sources = me - offsets
    previous = jnp.sum(jnp.where(piece_index[None, :] == sources[:, None], piece_lengths[None, :], 0), axis=1)
    table = jnp.concatenate([lengths[:1], previous, levels[:1]]).astype(jnp.int32)
    return attend(table, queries, kv, from_mixed, from_two, from_swap, gathered, gate_table)


def solution(mesh):
    return jax.shard_map(
        body,
        mesh=mesh,
        in_specs=(
            P(("videos", "group"), None),
            P(("videos", "group"), None),
            P(("videos", "group"), None),
            P(("videos", "group"), None),
            P(("videos", "group"), None),
            P(("videos", "group")),
            P(("videos", "group")),
            P(),
        ),
        out_specs=P(("videos", "group"), None),
        check_vma=False,
    )
```

```python
import functools
import math

import jax
import jax.numpy as jnp
from jax import lax
from jax.experimental import pallas as pl
from jax.experimental.pallas import tpu as pltpu
from jax.sharding import PartitionSpec as P

HEAD_DIM = 128
WIN = 4
HEADS_PER_STEP = 4


def partial_kernel(table_ref, q_ref, k0, v0, k2, v2, k3, v3, ck, cv, m_ref, l_ref, acc_ref, *, heads):
    scale = 1.0 / math.sqrt(HEAD_DIM)
    rows = q_ref.shape[0]
    slot = lax.broadcasted_iota(jnp.int32, (1, rows), 1)
    dims = (((1,), (1,)), ((), ()))
    blocks = ((k0, v0, 0), (k2, v2, 2), (k3, v3, 3))
    for h in range(heads):
        cols = slice(h * HEAD_DIM, (h + 1) * HEAD_DIM)
        q = q_ref[:, cols]
        scores = []
        for k_ref, _, j in blocks:
            s = jnp.dot(q, k_ref[:, cols], preferred_element_type=jnp.float32) * scale
            scores.append(jnp.where(slot < table_ref[j], s, -jnp.inf))
        scores.append(lax.dot_general(q, ck[:, cols], dims, preferred_element_type=jnp.float32) * scale)
        window = jnp.maximum(jnp.maximum(scores[0], scores[1]), scores[2])
        row_max = jnp.maximum(window.max(axis=1, keepdims=True), scores[3].max(axis=1, keepdims=True))
        values = [v_ref[:, cols] for _, v_ref, _ in blocks] + [cv[:, cols]]
        probabilities = [jnp.exp(s - row_max) for s in scores]
        window_sum = (probabilities[0] + probabilities[1]) + probabilities[2]
        denominator = window_sum.sum(axis=1, keepdims=True) + probabilities[3].sum(axis=1, keepdims=True)
        attended = jnp.zeros((rows, HEAD_DIM), jnp.float32)
        for p, v in zip(probabilities, values):
            attended = attended + jnp.dot(p.astype(jnp.bfloat16), v, preferred_element_type=jnp.float32)
        m_ref[:, h:h + 1] = row_max
        l_ref[:, h:h + 1] = denominator
        acc_ref[:, cols] = attended


def finish_kernel(table_ref, q_ref, k1, v1, m_ref, l_ref, acc_ref, gate_ref, o_ref, *, heads):
    scale = 1.0 / math.sqrt(HEAD_DIM)
    rows = q_ref.shape[0]
    slot = lax.broadcasted_iota(jnp.int32, (1, rows), 1)
    row = lax.broadcasted_iota(jnp.int32, (rows, 1), 0)
    gate = gate_ref[pl.ds(table_ref[4], 1), :]
    live_row = row < table_ref[0]
    for h in range(heads):
        cols = slice(h * HEAD_DIM, (h + 1) * HEAD_DIM)
        s = jnp.dot(q_ref[:, cols], k1[:, cols], preferred_element_type=jnp.float32) * scale
        s = jnp.where(slot < table_ref[1], s, -jnp.inf)
        old_max = m_ref[:, h:h + 1]
        new_max = jnp.maximum(old_max, s.max(axis=1, keepdims=True))
        rescale = jnp.exp(old_max - new_max)
        p = jnp.exp(s - new_max)
        denominator = l_ref[:, h:h + 1] * rescale + p.sum(axis=1, keepdims=True)
        attended = acc_ref[:, cols] * rescale + jnp.dot(p.astype(jnp.bfloat16), v1[:, cols], preferred_element_type=jnp.float32)
        attended = attended / denominator
        o_ref[:, cols] = jnp.where(live_row, attended * gate[:, cols], 0.0).astype(o_ref.dtype)


def attend(table, queries, kv_own, kv_a, kv_b, kv_c, cache, gate_table):
    rows, feat = queries.shape
    width = HEADS_PER_STEP * HEAD_DIM
    steps = feat // width
    cache_rows = cache.shape[0]
    levels = gate_table.shape[0]
    row_block = pl.BlockSpec((rows, width), lambda h, t: (0, h))
    k_block = pl.BlockSpec((None, rows, width), lambda h, t: (0, 0, h))
    v_block = pl.BlockSpec((None, rows, width), lambda h, t: (1, 0, h))
    cache_k_block = pl.BlockSpec((cache_rows, width), lambda h, t: (0, h))
    cache_v_block = pl.BlockSpec((cache_rows, width), lambda h, t: (0, steps + h))
    gate_block = pl.BlockSpec((levels, width), lambda h, t: (0, h))
    stat_block = pl.BlockSpec((None, rows, HEADS_PER_STEP), lambda h, t: (h, 0, 0))
    stat_shape = jax.ShapeDtypeStruct((steps, rows, HEADS_PER_STEP), jnp.float32)
    keys = 3 * rows + cache_rows
    m, l, acc = pl.pallas_call(
        functools.partial(partial_kernel, heads=HEADS_PER_STEP),
        out_shape=(stat_shape, stat_shape, jax.ShapeDtypeStruct((rows, feat), jnp.float32)),
        grid_spec=pltpu.PrefetchScalarGridSpec(
            num_scalar_prefetch=1,
            grid=(steps,),
            in_specs=[row_block, k_block, v_block, k_block, v_block, k_block, v_block, cache_k_block, cache_v_block],
            out_specs=(stat_block, stat_block, row_block),
        ),
        cost_estimate=pl.CostEstimate(
            flops=4 * rows * keys * feat,
            transcendentals=rows * keys * (feat // HEAD_DIM),
            bytes_accessed=2 * (7 * rows * feat + 2 * cache_rows * feat) + 4 * rows * feat,
        ),
    )(table, queries, kv_own, kv_own, kv_b, kv_b, kv_c, kv_c, cache, cache)
    return pl.pallas_call(
        functools.partial(finish_kernel, heads=HEADS_PER_STEP),
        out_shape=jax.ShapeDtypeStruct((rows, feat), jnp.bfloat16),
        grid_spec=pltpu.PrefetchScalarGridSpec(
            num_scalar_prefetch=1,
            grid=(steps,),
            in_specs=[row_block, k_block, v_block, stat_block, stat_block, row_block, gate_block],
            out_specs=row_block,
        ),
        cost_estimate=pl.CostEstimate(
            flops=4 * rows * rows * feat,
            transcendentals=rows * rows * (feat // HEAD_DIM),
            bytes_accessed=2 * (4 * rows * feat) + 4 * rows * feat + 4 * levels * feat,
        ),
    )(table, queries, kv_a, kv_a, m, l, acc, gate_table)


def gather_pieces(piece, size):
    if size & (size - 1):
        return lax.all_gather(piece, "group", axis=0, tiled=True)
    held = piece
    step = size // 2
    while step >= 1:
        other = lax.ppermute(held, "group", [(i, i ^ step) for i in range(size)])
        held = jnp.concatenate([held, other], 0)
        step //= 2
    return held


def body(queries, fresh_keys, fresh_values, cache_keys, cache_values, lengths, levels, gate_table):
    row_count, feat_width = queries.shape
    size = lax.axis_size("group")
    me = lax.axis_index("group")

    cache_rows = cache_keys.shape[0]
    tag = jnp.zeros((cache_rows, HEAD_DIM), jnp.bfloat16)
    tag = tag.at[0, 0].set(lengths[0].astype(jnp.bfloat16)).at[0, 1].set(me.astype(jnp.bfloat16))
    packed = jnp.concatenate([cache_keys, cache_values, tag], 1)
    gathered = gather_pieces(packed, size)
    piece_lengths = gathered[:, 2 * feat_width].astype(jnp.int32)
    piece_index = gathered[:, 2 * feat_width + 1].astype(jnp.int32)

    head_count = feat_width // HEAD_DIM
    keys_by_head = fresh_keys.reshape(row_count, head_count, HEAD_DIM).transpose(2, 1, 0).reshape(HEAD_DIM, head_count * row_count)
    kv = jnp.stack([keys_by_head, fresh_values], 0)
    pairs_two = [(i, i + 2) for i in range(size - 2)]
    pairs_mixed = [(i, i + 1) for i in range(0, size - 1, 2)] + [(i, i + 3) for i in range(1, size - 3, 2)]
    from_two = lax.ppermute(kv, "group", pairs_two)
    from_mixed = lax.ppermute(kv, "group", pairs_mixed)
    pairs_swap = [(i, i ^ 1) for i in range(size)]
    from_swap = lax.ppermute(from_two, "group", pairs_swap)

    odd = (me % 2) == 1
    offsets = jnp.where(odd, jnp.array([1, 2, 3], jnp.int32), jnp.array([3, 2, 1], jnp.int32))
    sources = me - offsets
    previous = jnp.sum(jnp.where(piece_index[None, :] == sources[:, None], piece_lengths[None, :], 0), axis=1)
    table = jnp.concatenate([lengths[:1], previous, levels[:1]]).astype(jnp.int32)
    return attend(table, queries, kv, from_mixed, from_two, from_swap, gathered, gate_table)


def solution(mesh):
    return jax.shard_map(
        body,
        mesh=mesh,
        in_specs=(
            P(("videos", "group"), None),
            P(("videos", "group"), None),
            P(("videos", "group"), None),
            P(("videos", "group"), None),
            P(("videos", "group"), None),
            P(("videos", "group")),
            P(("videos", "group")),
            P(),
        ),
        out_specs=P(("videos", "group"), None),
        check_vma=False,
    )
```

```python
import functools
import math

import jax
import jax.numpy as jnp
from jax import lax
from jax.experimental import pallas as pl
from jax.experimental.pallas import tpu as pltpu
from jax.sharding import PartitionSpec as P

HEAD_DIM = 128
WIN = 4
HEADS_PER_STEP = 8


def attention_kernel(table_ref, q_ref, k0, v0, k1, v1, k2, v2, k3, v3, ck, cv, gate_ref, o_ref, *, heads):
    scale = 1.0 / math.sqrt(HEAD_DIM)
    rows = q_ref.shape[0]
    slot = lax.broadcasted_iota(jnp.int32, (1, rows), 1)
    row = lax.broadcasted_iota(jnp.int32, (rows, 1), 0)
    level = table_ref[4]
    gate = gate_ref[pl.ds(level, 1), :]
    live_row = row < table_ref[0]
    blocks = ((k0, v0), (k1, v1), (k2, v2), (k3, v3))
    dims = (((1,), (1,)), ((), ()))
    head_cols = [slice(h * HEAD_DIM, (h + 1) * HEAD_DIM) for h in range(heads)]
    all_scores = []
    for cols in head_cols:
        q = q_ref[:, cols]
        scores = []
        for j, (k_ref, _) in enumerate(blocks):
            s = jnp.dot(q, k_ref[:, cols], preferred_element_type=jnp.float32) * scale
            scores.append(jnp.where(slot < table_ref[j], s, -jnp.inf))
        scores.append(lax.dot_general(q, ck[:, cols], dims, preferred_element_type=jnp.float32) * scale)
        all_scores.append(scores)
    all_probabilities = []
    all_denominators = []
    for scores in all_scores:
        window = jnp.maximum(jnp.maximum(scores[0], scores[1]), jnp.maximum(scores[2], scores[3]))
        row_max = jnp.maximum(window.max(axis=1, keepdims=True), scores[4].max(axis=1, keepdims=True))
        probabilities = [jnp.exp(s - row_max) for s in scores]
        window_sum = (probabilities[0] + probabilities[1]) + (probabilities[2] + probabilities[3])
        all_denominators.append(window_sum.sum(axis=1, keepdims=True) + probabilities[4].sum(axis=1, keepdims=True))
        all_probabilities.append([p.astype(jnp.bfloat16) for p in probabilities])
    for cols, weights, denominator in zip(head_cols, all_probabilities, all_denominators):
        values = [v_ref for _, v_ref in blocks] + [cv]
        attended = jnp.zeros((rows, HEAD_DIM), jnp.float32)
        for w, v_ref in zip(weights, values):
            attended = attended + jnp.dot(w, v_ref[:, cols], preferred_element_type=jnp.float32)
        attended = attended / denominator
        out = jnp.where(live_row, attended * gate[:, cols], 0.0)
        o_ref[:, cols] = out.astype(o_ref.dtype)


def attend(table, queries, kv_own, kv_a, kv_b, kv_c, cache, gate_table):
    rows, feat = queries.shape
    width = HEADS_PER_STEP * HEAD_DIM
    steps = feat // width
    cache_rows = cache.shape[0]
    levels = gate_table.shape[0]
    row_block = pl.BlockSpec((rows, width), lambda h, t: (0, h))
    k_block = pl.BlockSpec((None, rows, width), lambda h, t: (0, 0, h))
    v_block = pl.BlockSpec((None, rows, width), lambda h, t: (1, 0, h))
    cache_k_block = pl.BlockSpec((cache_rows, width), lambda h, t: (0, h))
    cache_v_block = pl.BlockSpec((cache_rows, width), lambda h, t: (0, steps + h))
    gate_block = pl.BlockSpec((levels, width), lambda h, t: (0, h))
    grid_spec = pltpu.PrefetchScalarGridSpec(
        num_scalar_prefetch=1,
        grid=(steps,),
        in_specs=[row_block, k_block, v_block, k_block, v_block, k_block, v_block, k_block, v_block,
                  cache_k_block, cache_v_block, gate_block],
        out_specs=row_block,
    )
    keys = 4 * rows + cache_rows
    cost = pl.CostEstimate(
        flops=4 * rows * keys * feat,
        transcendentals=rows * keys * (feat // HEAD_DIM),
        bytes_accessed=2 * (2 * rows * feat + 8 * rows * feat + 2 * cache_rows * feat) + 4 * levels * feat,
    )
    return pl.pallas_call(
        functools.partial(attention_kernel, heads=HEADS_PER_STEP),
        out_shape=jax.ShapeDtypeStruct((rows, feat), jnp.bfloat16),
        grid_spec=grid_spec,
        cost_estimate=cost,
    )(table, queries, kv_own, kv_own, kv_a, kv_a, kv_b, kv_b, kv_c, kv_c, cache, cache, gate_table)


def gather_pieces(piece, size):
    if size & (size - 1):
        return lax.all_gather(piece, "group", axis=0, tiled=True)
    held = piece
    step = size // 2
    while step >= 1:
        other = lax.ppermute(held, "group", [(i, i ^ step) for i in range(size)])
        held = jnp.concatenate([held, other], 0)
        step //= 2
    return held


def body(queries, fresh_keys, fresh_values, cache_keys, cache_values, lengths, levels, gate_table):
    row_count, feat_width = queries.shape
    size = lax.axis_size("group")
    me = lax.axis_index("group")

    cache_rows = cache_keys.shape[0]
    tag = jnp.zeros((cache_rows, HEAD_DIM), jnp.bfloat16)
    tag = tag.at[0, 0].set(lengths[0].astype(jnp.bfloat16)).at[0, 1].set(me.astype(jnp.bfloat16))
    packed = jnp.concatenate([cache_keys, cache_values, tag], 1)
    gathered = gather_pieces(packed, size)
    piece_lengths = gathered[:, 2 * feat_width].astype(jnp.int32)
    piece_index = gathered[:, 2 * feat_width + 1].astype(jnp.int32)

    head_count = feat_width // HEAD_DIM
    keys_by_head = fresh_keys.reshape(row_count, head_count, HEAD_DIM).transpose(2, 1, 0).reshape(HEAD_DIM, head_count * row_count)
    kv = jnp.stack([keys_by_head, fresh_values], 0)
    pairs_two = [(i, i + 2) for i in range(size - 2)]
    pairs_mixed = [(i, i + 1) for i in range(0, size - 1, 2)] + [(i, i + 3) for i in range(1, size - 3, 2)]
    from_two = lax.ppermute(kv, "group", pairs_two)
    from_mixed = lax.ppermute(kv, "group", pairs_mixed)
    pairs_swap = [(i, i ^ 1) for i in range(size)]
    from_swap = lax.ppermute(from_two, "group", pairs_swap)

    odd = (me % 2) == 1
    offsets = jnp.where(odd, jnp.array([1, 2, 3], jnp.int32), jnp.array([3, 2, 1], jnp.int32))
    sources = me - offsets
    previous = jnp.sum(jnp.where(piece_index[None, :] == sources[:, None], piece_lengths[None, :], 0), axis=1)
    table = jnp.concatenate([lengths[:1], previous, levels[:1]]).astype(jnp.int32)
    return attend(table, queries, kv, from_mixed, from_two, from_swap, gathered, gate_table)


def solution(mesh):
    return jax.shard_map(
        body,
        mesh=mesh,
        in_specs=(
            P(("videos", "group"), None),
            P(("videos", "group"), None),
            P(("videos", "group"), None),
            P(("videos", "group"), None),
            P(("videos", "group"), None),
            P(("videos", "group")),
            P(("videos", "group")),
            P(),
        ),
        out_specs=P(("videos", "group"), None),
        check_vma=False,
    )
```

```python
import functools
import math

import jax
import jax.numpy as jnp
from jax import lax
from jax.experimental import pallas as pl
from jax.experimental.pallas import tpu as pltpu
from jax.sharding import PartitionSpec as P

HEAD_DIM = 128
WIN = 4
HEADS_PER_STEP = 12


def attention_kernel(table_ref, q_ref, k0, v0, k1, v1, k2, v2, k3, v3, ck, cv, gate_ref, o_ref, *, heads):
    scale = 1.0 / math.sqrt(HEAD_DIM)
    rows = q_ref.shape[0]
    slot = lax.broadcasted_iota(jnp.int32, (1, rows), 1)
    row = lax.broadcasted_iota(jnp.int32, (rows, 1), 0)
    level = table_ref[4]
    gate = gate_ref[pl.ds(level, 1), :]
    live_row = row < table_ref[0]
    blocks = ((k0, v0), (k1, v1), (k2, v2), (k3, v3))
    dims = (((1,), (1,)), ((), ()))
    head_cols = [slice(h * HEAD_DIM, (h + 1) * HEAD_DIM) for h in range(heads)]
    all_scores = []
    for cols in head_cols:
        q = q_ref[:, cols]
        scores = []
        for j, (k_ref, _) in enumerate(blocks):
            s = jnp.dot(q, k_ref[:, cols], preferred_element_type=jnp.float32) * scale
            scores.append(jnp.where(slot < table_ref[j], s, -jnp.inf))
        scores.append(lax.dot_general(q, ck[:, cols], dims, preferred_element_type=jnp.float32) * scale)
        all_scores.append(scores)
    all_probabilities = []
    all_denominators = []
    for scores in all_scores:
        window = jnp.maximum(jnp.maximum(scores[0], scores[1]), jnp.maximum(scores[2], scores[3]))
        row_max = jnp.maximum(window.max(axis=1, keepdims=True), scores[4].max(axis=1, keepdims=True))
        probabilities = [jnp.exp(s - row_max) for s in scores]
        window_sum = (probabilities[0] + probabilities[1]) + (probabilities[2] + probabilities[3])
        all_denominators.append(window_sum.sum(axis=1, keepdims=True) + probabilities[4].sum(axis=1, keepdims=True))
        all_probabilities.append([p.astype(jnp.bfloat16) for p in probabilities])
    for cols, weights, denominator in zip(head_cols, all_probabilities, all_denominators):
        values = [v_ref for _, v_ref in blocks] + [cv]
        attended = jnp.zeros((rows, HEAD_DIM), jnp.float32)
        for w, v_ref in zip(weights, values):
            attended = attended + jnp.dot(w, v_ref[:, cols], preferred_element_type=jnp.float32)
        attended = attended / denominator
        out = jnp.where(live_row, attended * gate[:, cols], 0.0)
        o_ref[:, cols] = out.astype(o_ref.dtype)


def attend(table, queries, kv_own, kv_a, kv_b, kv_c, cache, gate_table):
    rows, feat = queries.shape
    width = HEADS_PER_STEP * HEAD_DIM
    steps = feat // width
    cache_rows = cache.shape[0]
    levels = gate_table.shape[0]
    row_block = pl.BlockSpec((rows, width), lambda h, t: (0, h))
    k_block = pl.BlockSpec((None, rows, width), lambda h, t: (0, 0, h))
    v_block = pl.BlockSpec((None, rows, width), lambda h, t: (1, 0, h))
    cache_k_block = pl.BlockSpec((cache_rows, width), lambda h, t: (0, h))
    cache_v_block = pl.BlockSpec((cache_rows, width), lambda h, t: (0, steps + h))
    gate_block = pl.BlockSpec((levels, width), lambda h, t: (0, h))
    grid_spec = pltpu.PrefetchScalarGridSpec(
        num_scalar_prefetch=1,
        grid=(steps,),
        in_specs=[row_block, k_block, v_block, k_block, v_block, k_block, v_block, k_block, v_block,
                  cache_k_block, cache_v_block, gate_block],
        out_specs=row_block,
    )
    keys = 4 * rows + cache_rows
    cost = pl.CostEstimate(
        flops=4 * rows * keys * feat,
        transcendentals=rows * keys * (feat // HEAD_DIM),
        bytes_accessed=2 * (2 * rows * feat + 8 * rows * feat + 2 * cache_rows * feat) + 4 * levels * feat,
    )
    return pl.pallas_call(
        functools.partial(attention_kernel, heads=HEADS_PER_STEP),
        out_shape=jax.ShapeDtypeStruct((rows, feat), jnp.bfloat16),
        grid_spec=grid_spec,
        cost_estimate=cost,
    )(table, queries, kv_own, kv_own, kv_a, kv_a, kv_b, kv_b, kv_c, kv_c, cache, cache, gate_table)


def gather_pieces(piece, size):
    if size & (size - 1):
        return lax.all_gather(piece, "group", axis=0, tiled=True)
    held = piece
    step = size // 2
    while step >= 1:
        other = lax.ppermute(held, "group", [(i, i ^ step) for i in range(size)])
        held = jnp.concatenate([held, other], 0)
        step //= 2
    return held


def body(queries, fresh_keys, fresh_values, cache_keys, cache_values, lengths, levels, gate_table):
    row_count, feat_width = queries.shape
    size = lax.axis_size("group")
    me = lax.axis_index("group")

    cache_rows = cache_keys.shape[0]
    tag = jnp.zeros((cache_rows, HEAD_DIM), jnp.bfloat16)
    tag = tag.at[0, 0].set(lengths[0].astype(jnp.bfloat16)).at[0, 1].set(me.astype(jnp.bfloat16))
    packed = jnp.concatenate([cache_keys, cache_values, tag], 1)
    gathered = gather_pieces(packed, size)
    piece_lengths = gathered[:, 2 * feat_width].astype(jnp.int32)
    piece_index = gathered[:, 2 * feat_width + 1].astype(jnp.int32)

    head_count = feat_width // HEAD_DIM
    keys_by_head = fresh_keys.reshape(row_count, head_count, HEAD_DIM).transpose(2, 1, 0).reshape(HEAD_DIM, head_count * row_count)
    kv = jnp.stack([keys_by_head, fresh_values], 0)
    pairs_two = [(i, i + 2) for i in range(size - 2)]
    pairs_mixed = [(i, i + 1) for i in range(0, size - 1, 2)] + [(i, i + 3) for i in range(1, size - 3, 2)]
    from_two = lax.ppermute(kv, "group", pairs_two)
    from_mixed = lax.ppermute(kv, "group", pairs_mixed)
    pairs_swap = [(i, i ^ 1) for i in range(size)]
    from_swap = lax.ppermute(from_two, "group", pairs_swap)

    odd = (me % 2) == 1
    offsets = jnp.where(odd, jnp.array([1, 2, 3], jnp.int32), jnp.array([3, 2, 1], jnp.int32))
    sources = me - offsets
    previous = jnp.sum(jnp.where(piece_index[None, :] == sources[:, None], piece_lengths[None, :], 0), axis=1)
    table = jnp.concatenate([lengths[:1], previous, levels[:1]]).astype(jnp.int32)
    return attend(table, queries, kv, from_mixed, from_two, from_swap, gathered, gate_table)


def solution(mesh):
    return jax.shard_map(
        body,
        mesh=mesh,
        in_specs=(
            P(("videos", "group"), None),
            P(("videos", "group"), None),
            P(("videos", "group"), None),
            P(("videos", "group"), None),
            P(("videos", "group"), None),
            P(("videos", "group")),
            P(("videos", "group")),
            P(),
        ),
        out_specs=P(("videos", "group"), None),
        check_vma=False,
    )
```

```python
import functools
import math

import jax
import jax.numpy as jnp
from jax import lax
from jax.experimental import pallas as pl
from jax.experimental.pallas import tpu as pltpu
from jax.sharding import PartitionSpec as P

HEAD_DIM = 128
WIN = 4
HEADS_PER_STEP = 24


def attention_kernel(table_ref, q_ref, k0, v0, k1, v1, k2, v2, k3, v3, ck, cv, gate_ref, o_ref, *, heads):
    scale = 1.0 / math.sqrt(HEAD_DIM)
    rows = q_ref.shape[0]
    slot = lax.broadcasted_iota(jnp.int32, (1, rows), 1)
    row = lax.broadcasted_iota(jnp.int32, (rows, 1), 0)
    level = table_ref[4]
    gate = gate_ref[pl.ds(level, 1), :]
    live_row = row < table_ref[0]
    blocks = ((k0, v0), (k1, v1), (k2, v2), (k3, v3))
    dims = (((1,), (1,)), ((), ()))
    head_cols = [slice(h * HEAD_DIM, (h + 1) * HEAD_DIM) for h in range(heads)]
    all_scores = []
    for cols in head_cols:
        q = q_ref[:, cols]
        scores = []
        for j, (k_ref, _) in enumerate(blocks):
            s = jnp.dot(q, k_ref[:, cols], preferred_element_type=jnp.float32) * scale
            scores.append(jnp.where(slot < table_ref[j], s, -jnp.inf))
        scores.append(lax.dot_general(q, ck[:, cols], dims, preferred_element_type=jnp.float32) * scale)
        all_scores.append(scores)
    all_probabilities = []
    all_denominators = []
    for scores in all_scores:
        window = jnp.maximum(jnp.maximum(scores[0], scores[1]), jnp.maximum(scores[2], scores[3]))
        row_max = jnp.maximum(window.max(axis=1, keepdims=True), scores[4].max(axis=1, keepdims=True))
        probabilities = [jnp.exp(s - row_max) for s in scores]
        window_sum = (probabilities[0] + probabilities[1]) + (probabilities[2] + probabilities[3])
        all_denominators.append(window_sum.sum(axis=1, keepdims=True) + probabilities[4].sum(axis=1, keepdims=True))
        all_probabilities.append([p.astype(jnp.bfloat16) for p in probabilities])
    for cols, weights, denominator in zip(head_cols, all_probabilities, all_denominators):
        values = [v_ref for _, v_ref in blocks] + [cv]
        attended = jnp.zeros((rows, HEAD_DIM), jnp.float32)
        for w, v_ref in zip(weights, values):
            attended = attended + jnp.dot(w, v_ref[:, cols], preferred_element_type=jnp.float32)
        attended = attended / denominator
        out = jnp.where(live_row, attended * gate[:, cols], 0.0)
        o_ref[:, cols] = out.astype(o_ref.dtype)


def attend(table, queries, kv_own, kv_a, kv_b, kv_c, cache, gate_table):
    rows, feat = queries.shape
    width = HEADS_PER_STEP * HEAD_DIM
    steps = feat // width
    cache_rows = cache.shape[0]
    levels = gate_table.shape[0]
    row_block = pl.BlockSpec((rows, width), lambda h, t: (0, h))
    k_block = pl.BlockSpec((None, rows, width), lambda h, t: (0, 0, h))
    v_block = pl.BlockSpec((None, rows, width), lambda h, t: (1, 0, h))
    cache_k_block = pl.BlockSpec((cache_rows, width), lambda h, t: (0, h))
    cache_v_block = pl.BlockSpec((cache_rows, width), lambda h, t: (0, steps + h))
    gate_block = pl.BlockSpec((levels, width), lambda h, t: (0, h))
    grid_spec = pltpu.PrefetchScalarGridSpec(
        num_scalar_prefetch=1,
        grid=(steps,),
        in_specs=[row_block, k_block, v_block, k_block, v_block, k_block, v_block, k_block, v_block,
                  cache_k_block, cache_v_block, gate_block],
        out_specs=row_block,
    )
    keys = 4 * rows + cache_rows
    cost = pl.CostEstimate(
        flops=4 * rows * keys * feat,
        transcendentals=rows * keys * (feat // HEAD_DIM),
        bytes_accessed=2 * (2 * rows * feat + 8 * rows * feat + 2 * cache_rows * feat) + 4 * levels * feat,
    )
    return pl.pallas_call(
        functools.partial(attention_kernel, heads=HEADS_PER_STEP),
        out_shape=jax.ShapeDtypeStruct((rows, feat), jnp.bfloat16),
        grid_spec=grid_spec,
        cost_estimate=cost,
    )(table, queries, kv_own, kv_own, kv_a, kv_a, kv_b, kv_b, kv_c, kv_c, cache, cache, gate_table)


def gather_pieces(piece, size):
    if size & (size - 1):
        return lax.all_gather(piece, "group", axis=0, tiled=True)
    held = piece
    step = size // 2
    while step >= 1:
        other = lax.ppermute(held, "group", [(i, i ^ step) for i in range(size)])
        held = jnp.concatenate([held, other], 0)
        step //= 2
    return held


def body(queries, fresh_keys, fresh_values, cache_keys, cache_values, lengths, levels, gate_table):
    row_count, feat_width = queries.shape
    size = lax.axis_size("group")
    me = lax.axis_index("group")

    cache_rows = cache_keys.shape[0]
    tag = jnp.zeros((cache_rows, HEAD_DIM), jnp.bfloat16)
    tag = tag.at[0, 0].set(lengths[0].astype(jnp.bfloat16)).at[0, 1].set(me.astype(jnp.bfloat16))
    packed = jnp.concatenate([cache_keys, cache_values, tag], 1)
    gathered = gather_pieces(packed, size)
    piece_lengths = gathered[:, 2 * feat_width].astype(jnp.int32)
    piece_index = gathered[:, 2 * feat_width + 1].astype(jnp.int32)

    head_count = feat_width // HEAD_DIM
    keys_by_head = fresh_keys.reshape(row_count, head_count, HEAD_DIM).transpose(2, 1, 0).reshape(HEAD_DIM, head_count * row_count)
    kv = jnp.stack([keys_by_head, fresh_values], 0)
    pairs_two = [(i, i + 2) for i in range(size - 2)]
    pairs_mixed = [(i, i + 1) for i in range(0, size - 1, 2)] + [(i, i + 3) for i in range(1, size - 3, 2)]
    from_two = lax.ppermute(kv, "group", pairs_two)
    from_mixed = lax.ppermute(kv, "group", pairs_mixed)
    pairs_swap = [(i, i ^ 1) for i in range(size)]
    from_swap = lax.ppermute(from_two, "group", pairs_swap)

    odd = (me % 2) == 1
    offsets = jnp.where(odd, jnp.array([1, 2, 3], jnp.int32), jnp.array([3, 2, 1], jnp.int32))
    sources = me - offsets
    previous = jnp.sum(jnp.where(piece_index[None, :] == sources[:, None], piece_lengths[None, :], 0), axis=1)
    table = jnp.concatenate([lengths[:1], previous, levels[:1]]).astype(jnp.int32)
    return attend(table, queries, kv, from_mixed, from_two, from_swap, gathered, gate_table)


def solution(mesh):
    return jax.shard_map(
        body,
        mesh=mesh,
        in_specs=(
            P(("videos", "group"), None),
            P(("videos", "group"), None),
            P(("videos", "group"), None),
            P(("videos", "group"), None),
            P(("videos", "group"), None),
            P(("videos", "group")),
            P(("videos", "group")),
            P(),
        ),
        out_specs=P(("videos", "group"), None),
        check_vma=False,
    )
```

```python
import functools
import math

import jax
import jax.numpy as jnp
from jax import lax
from jax.experimental import pallas as pl
from jax.experimental.pallas import tpu as pltpu
from jax.sharding import PartitionSpec as P

HEAD_DIM = 128
WIN = 4
HEADS_PER_STEP = 6


def attention_kernel(table_ref, q_ref, k0, v0, k1, v1, k2, v2, k3, v3, ck, cv, gate_ref, o_ref, *, heads):
    scale = 1.0 / math.sqrt(HEAD_DIM)
    rows = q_ref.shape[0]
    slot = lax.broadcasted_iota(jnp.int32, (1, rows), 1)
    row = lax.broadcasted_iota(jnp.int32, (rows, 1), 0)
    level = table_ref[4]
    gate = gate_ref[pl.ds(level, 1), :]
    live_row = row < table_ref[0]
    blocks = ((k0, v0), (k1, v1), (k2, v2), (k3, v3))
    dims = (((1,), (1,)), ((), ()))
    head_cols = [slice(h * HEAD_DIM, (h + 1) * HEAD_DIM) for h in range(heads)]
    all_scores = []
    for cols in head_cols:
        q = q_ref[:, cols]
        scores = []
        for j, (k_ref, _) in enumerate(blocks):
            s = jnp.dot(q, k_ref[:, cols], preferred_element_type=jnp.float32) * scale
            scores.append(jnp.where(slot < table_ref[j], s, -jnp.inf))
        scores.append(lax.dot_general(q, ck[:, cols], dims, preferred_element_type=jnp.float32) * scale)
        all_scores.append(scores)
    all_probabilities = []
    all_denominators = []
    for scores in all_scores:
        window = jnp.maximum(jnp.maximum(scores[0], scores[1]), jnp.maximum(scores[2], scores[3]))
        row_max = jnp.maximum(window.max(axis=1, keepdims=True), scores[4].max(axis=1, keepdims=True))
        probabilities = [jnp.exp(s - row_max) for s in scores]
        window_sum = (probabilities[0] + probabilities[1]) + (probabilities[2] + probabilities[3])
        all_denominators.append(window_sum.sum(axis=1, keepdims=True) + probabilities[4].sum(axis=1, keepdims=True))
        all_probabilities.append([p.astype(jnp.bfloat16) for p in probabilities])
    for cols, weights, denominator in zip(head_cols, all_probabilities, all_denominators):
        values = [v_ref for _, v_ref in blocks] + [cv]
        attended = jnp.zeros((rows, HEAD_DIM), jnp.float32)
        for w, v_ref in zip(weights, values):
            attended = attended + jnp.dot(w, v_ref[:, cols], preferred_element_type=jnp.float32)
        attended = attended / denominator
        out = jnp.where(live_row, attended * gate[:, cols], 0.0)
        o_ref[:, cols] = out.astype(o_ref.dtype)


def attend(table, queries, kv_own, kv_a, kv_b, kv_c, cache, gate_table):
    rows, feat = queries.shape
    width = HEADS_PER_STEP * HEAD_DIM
    steps = feat // width
    cache_rows = cache.shape[0]
    levels = gate_table.shape[0]
    row_block = pl.BlockSpec((rows, width), lambda h, t: (0, h))
    k_block = pl.BlockSpec((None, rows, width), lambda h, t: (0, 0, h))
    v_block = pl.BlockSpec((None, rows, width), lambda h, t: (1, 0, h))
    cache_k_block = pl.BlockSpec((cache_rows, width), lambda h, t: (0, h))
    cache_v_block = pl.BlockSpec((cache_rows, width), lambda h, t: (0, steps + h))
    gate_block = pl.BlockSpec((levels, width), lambda h, t: (0, h))
    grid_spec = pltpu.PrefetchScalarGridSpec(
        num_scalar_prefetch=1,
        grid=(steps,),
        in_specs=[row_block, k_block, v_block, k_block, v_block, k_block, v_block, k_block, v_block,
                  cache_k_block, cache_v_block, gate_block],
        out_specs=row_block,
    )
    keys = 4 * rows + cache_rows
    cost = pl.CostEstimate(
        flops=4 * rows * keys * feat,
        transcendentals=rows * keys * (feat // HEAD_DIM),
        bytes_accessed=2 * (2 * rows * feat + 8 * rows * feat + 2 * cache_rows * feat) + 4 * levels * feat,
    )
    return pl.pallas_call(
        functools.partial(attention_kernel, heads=HEADS_PER_STEP),
        out_shape=jax.ShapeDtypeStruct((rows, feat), jnp.bfloat16),
        grid_spec=grid_spec,
        cost_estimate=cost,
    )(table, queries, kv_own, kv_own, kv_a, kv_a, kv_b, kv_b, kv_c, kv_c, cache, cache, gate_table)


def gather_pieces(piece, size):
    if size & (size - 1):
        return lax.all_gather(piece, "group", axis=0, tiled=True)
    held = piece
    step = size // 2
    while step >= 1:
        other = lax.ppermute(held, "group", [(i, i ^ step) for i in range(size)])
        held = jnp.concatenate([held, other], 0)
        step //= 2
    return held


def body(queries, fresh_keys, fresh_values, cache_keys, cache_values, lengths, levels, gate_table):
    row_count, feat_width = queries.shape
    size = lax.axis_size("group")
    me = lax.axis_index("group")

    cache_rows = cache_keys.shape[0]
    tag = jnp.zeros((cache_rows, HEAD_DIM), jnp.bfloat16)
    tag = tag.at[0, 0].set(lengths[0].astype(jnp.bfloat16)).at[0, 1].set(me.astype(jnp.bfloat16))
    packed = jnp.concatenate([cache_keys, cache_values, tag], 1)
    gathered = gather_pieces(packed, size)
    piece_lengths = gathered[:, 2 * feat_width].astype(jnp.int32)
    piece_index = gathered[:, 2 * feat_width + 1].astype(jnp.int32)

    head_count = feat_width // HEAD_DIM
    keys_by_head = fresh_keys.reshape(row_count, head_count, HEAD_DIM).transpose(2, 1, 0).reshape(HEAD_DIM, head_count * row_count)
    kv = jnp.stack([keys_by_head, fresh_values], 0)
    pairs_two = [(i, i + 2) for i in range(size - 2)]
    pairs_mixed = [(i, i + 1) for i in range(0, size - 1, 2)] + [(i, i + 3) for i in range(1, size - 3, 2)]
    from_two = lax.ppermute(kv, "group", pairs_two)
    from_mixed = lax.ppermute(kv, "group", pairs_mixed)
    pairs_swap = [(i, i ^ 1) for i in range(size)]
    from_swap = lax.ppermute(from_two, "group", pairs_swap)

    odd = (me % 2) == 1
    offsets = jnp.where(odd, jnp.array([1, 2, 3], jnp.int32), jnp.array([3, 2, 1], jnp.int32))
    sources = me - offsets
    previous = jnp.sum(jnp.where(piece_index[None, :] == sources[:, None], piece_lengths[None, :], 0), axis=1)
    table = jnp.concatenate([lengths[:1], previous, levels[:1]]).astype(jnp.int32)
    return attend(table, queries, kv, from_mixed, from_two, from_swap, gathered, gate_table)


def solution(mesh):
    return jax.shard_map(
        body,
        mesh=mesh,
        in_specs=(
            P(("videos", "group"), None),
            P(("videos", "group"), None),
            P(("videos", "group"), None),
            P(("videos", "group"), None),
            P(("videos", "group"), None),
            P(("videos", "group")),
            P(("videos", "group")),
            P(),
        ),
        out_specs=P(("videos", "group"), None),
        check_vma=False,
    )
```
